128 devices in a mesh: dop: 8 (over y, core), rng: 16 (over x, z).
Axes of the slice: x: 4, y: 4, z: 4, core: 2. Of those that a mesh axis runs over, the one named last changes fastest.
Arguments:
- echoes: bfloat16 [8192, 2, 32, 128], P(('rng', 'dop')), may hold values from -60 to 60
- training: int32 [128, 8192], P('dop', 'rng'), may hold values 0 or 1
- look_index: int32 [64], replicated, may hold values from 0 to 255
Outputs:
- beam_output: float32 [128, 2, 64, 8192], P('dop', None, None, 'rng')
The draws below stay inside these ranges and needn't reach their ends.
All inputs are finite; a program needn't handle non-finite values. No bound on the sum of `training` on one device may be relied on, other than what follows from the above.
Results may differ from the reference program's by a relative error of at most 0.012.
The reference program's roundings to bfloat16 on the way (of `twiddle`, `spectra`, `snapshot` and `weights`) count: a program that leaves them out, or rounds other values in their place, can miss the bound.
Values may be sent and summed in bfloat16 or wider, within the bound.
No kernel may reach another device: no remote copies, remote signals or barrier semaphores. Data moves between devices by JAX's collectives and lax.ppermute only.
A program may use at most 64 MiB of HBM per device.

```python
import math
import jax
import jax.numpy as jnp
from jax import lax

CH = 32
PULSES = 128
LOOKS = 64
ANGLES = 256
DOPPLER = 128
RANGE = 8192
RANGE_DEV = 512
SNAP = 192


def draw_echoes(key, part):
    key_list = jax.random.split(key, 9)
    cell_ids = jnp.arange(RANGE).astype(jnp.float32)
    channel_ids = jnp.arange(CH).astype(jnp.float32)
    pulse_ids = jnp.arange(PULSES).astype(jnp.float32)
    range_trend = jnp.exp((1.0 - cell_ids / RANGE) * math.log(3.0))
    roughness = jnp.exp(jax.random.uniform(key_list[0], (RANGE,), jnp.float32, math.log(0.5), math.log(2.0)))
    amplitude = 0.5 * range_trend * roughness
    channel_gain = jnp.exp(jax.random.uniform(key_list[1], (CH,), jnp.float32, math.log(0.55), math.log(1.8)))
    noise_draw = jax.random.normal(key_list[2], (RANGE, 2, CH, PULSES), jnp.float32)
    clutter_low = 0.8
    clutter_high = 2.0
    real_sum = amplitude[:, None, None] * noise_draw[:, 0]
    imag_sum = amplitude[:, None, None] * noise_draw[:, 1]
    jammer_count = 12
    jammer_sines = -0.95 + 1.9 * (jnp.arange(jammer_count).astype(jnp.float32) + jax.random.uniform(key_list[3], (jammer_count,), jnp.float32, 0.2, 0.8)) / jammer_count
    jammer_levels = jnp.exp(jax.random.uniform(key_list[4], (jammer_count,), jnp.float32, math.log(0.5), math.log(5.0)))
    jammer_signal = jax.random.normal(key_list[5], (jammer_count, 2, RANGE, PULSES), jnp.float32)
    for jammer_id in range(jammer_count):
        phases = jnp.pi * channel_ids * jammer_sines[jammer_id]
        cos_phase = jnp.cos(phases)[None, :, None]
        sin_phase = jnp.sin(phases)[None, :, None]
        signal_real = jammer_signal[jammer_id, 0][:, None, :]
        signal_imag = jammer_signal[jammer_id, 1][:, None, :]
        real_sum = real_sum + jammer_levels[jammer_id] * (cos_phase * signal_real - sin_phase * signal_imag)
        imag_sum = imag_sum + jammer_levels[jammer_id] * (sin_phase * signal_real + cos_phase * signal_imag)
    patch_count = 4
    clutter_sines = jax.random.uniform(key_list[6], (RANGE, patch_count), jnp.float32, -1.0, 1.0)
    clutter_levels = amplitude[:, None] * jnp.exp(jax.random.uniform(key_list[7], (RANGE, patch_count), jnp.float32, math.log(clutter_low), math.log(clutter_high)))
    clutter_amps = jax.random.normal(key_list[8], (RANGE, patch_count, 2), jnp.float32)
    for patch_id in range(patch_count):
        sine_col = clutter_sines[:, patch_id][:, None, None]
        phase_grid = jnp.pi * channel_ids[None, :, None] * sine_col + 2.0 * jnp.pi * 0.49 * sine_col * pulse_ids[None, None, :]
        amp_real = (clutter_levels[:, patch_id] * clutter_amps[:, patch_id, 0])[:, None, None]
        amp_imag = (clutter_levels[:, patch_id] * clutter_amps[:, patch_id, 1])[:, None, None]
        cos_grid = jnp.cos(phase_grid)
        sin_grid = jnp.sin(phase_grid)
        real_sum = real_sum + amp_real * cos_grid - amp_imag * sin_grid
        imag_sum = imag_sum + amp_real * sin_grid + amp_imag * cos_grid
    values = jnp.stack([real_sum, imag_sum], axis=1) * channel_gain[None, None, :, None]
    return jnp.clip(values, -60.0, 60.0).astype(jnp.bfloat16)


def place_ends(values, stream_key, least, top_value):
    extent = values.shape
    index_at = [jax.random.randint(jax.random.fold_in(stream_key, axis), (), 0, extent[axis]) for axis in range(len(extent))]
    values = values.at[tuple(index_at)].set(least)
    longest = extent.index(max(extent))
    index_at[longest] = (index_at[longest] + 1) % extent[longest]
    return values.at[tuple(index_at)].set(top_value)


def setup_inputs(seed: int = 0) -> dict:
    streams_of = jax.random.split(jax.random.key(seed), 4)
    echoes = draw_echoes(jax.random.fold_in(streams_of[3], 71), 0)
    training = place_ends((jax.random.randint(streams_of[1], (DOPPLER, RANGE), 0, 4) < 3).astype(jnp.int32), jax.random.fold_in(streams_of[1], 1), 0, 1)
    look_index = place_ends(jax.random.randint(streams_of[2], (LOOKS,), 0, ANGLES), jax.random.fold_in(streams_of[2], 1), 0, ANGLES - 1).astype(jnp.int32)
    return {"echoes": echoes, "training": training, "look_index": look_index}


loading = 0.1
epsilon = 1e-06
highest = lax.Precision.HIGHEST

def twiddles():
    pulse_ids = jnp.arange(PULSES, dtype=jnp.int32)
    phase_ids = pulse_ids[:, None] * pulse_ids[None, :] % PULSES
    angles = phase_ids.astype(jnp.float32) * (2.0 * jnp.pi / PULSES)
    return jnp.concatenate([jnp.cos(angles), jnp.sin(angles)], axis=0).astype(jnp.bfloat16)

def doppler_block(echo_rows, twiddle):
    product = jnp.einsum('kp,rqcp->krqc', twiddle.astype(jnp.float32), echo_rows.astype(jnp.float32), precision=highest)
    cosine = product[:PULSES]
    sine = product[PULSES:]
    real_part = cosine[:, :, 0] + sine[:, :, 1]
    imag_part = cosine[:, :, 1] - sine[:, :, 0]
    return jnp.stack([real_part, imag_part], axis=2).reshape(PULSES, echo_rows.shape[0], 2 * CH).astype(jnp.bfloat16)

def steering(look_index):
    sines = -1.0 + (2.0 * look_index.astype(jnp.float32) + 1.0) / ANGLES
    channel_ids = jnp.arange(CH).astype(jnp.float32)
    phases = jnp.pi * channel_ids[:, None] * sines[None, :]
    zeros = jnp.zeros((CH, LOOKS), jnp.float32)
    return jnp.stack([zeros, zeros, jnp.cos(phases), jnp.sin(phases), zeros, zeros]).reshape(SNAP, LOOKS)

def full_matrix(gram_matrix):
    gram_grid = gram_matrix.reshape(3, 2, CH, 3, 2, CH)
    flipped = gram_grid[:, ::-1, :, :, ::-1, :]
    flip_sign = jnp.array([1.0, -1.0], jnp.float32)
    sign_grid = (flip_sign[:, None] * flip_sign[None, :]).reshape(1, 2, 1, 1, 2, 1)
    return (gram_grid + sign_grid * flipped).reshape(SNAP, SNAP)

def mvdr_weights(matrix, steer):
    bin_count = matrix.shape[0]
    power = jnp.trace(matrix, axis1=1, axis2=2) / SNAP + epsilon
    regular = matrix / power[:, None, None] + loading * jnp.eye(SNAP, dtype=jnp.float32)
    factor = jnp.linalg.cholesky(regular)
    targets = jnp.broadcast_to(steer, (bin_count, SNAP, LOOKS))
    forward = lax.linalg.triangular_solve(factor, targets, left_side=True, lower=True)
    solved = lax.linalg.triangular_solve(factor, forward, left_side=True, lower=True, transpose_a=True)
    gains = lax.optimization_barrier(jnp.sum(targets * solved, axis=1))
    unit = solved / jnp.sqrt(gains)[:, None, :]
    shaped = unit.reshape(bin_count, 3, 2, CH, LOOKS)
    rotated = jnp.stack([-shaped[:, :, 1], shaped[:, :, 0]], axis=2)
    return jnp.concatenate([unit, rotated.reshape(bin_count, SNAP, LOOKS)], axis=2).astype(jnp.bfloat16)

def reference(echoes, training, look_index):
    twiddle = twiddles()
    range_blocks = echoes.reshape(RANGE // RANGE_DEV, RANGE_DEV, 2, CH, PULSES)
    spectra_blocks = lax.map(lambda rows: doppler_block(rows, twiddle), range_blocks)
    spectra = jnp.transpose(spectra_blocks, (1, 0, 2, 3)).reshape(DOPPLER, RANGE, 2 * CH)
    steer = steering(look_index)

    def one_bin(bin_id):
        neighbours = ((bin_id + jnp.arange(3, dtype=jnp.int32) - 1 + DOPPLER) % DOPPLER).astype(jnp.int32)
        picked = jnp.take(spectra, neighbours, axis=0)
        snapshot = jnp.transpose(picked, (1, 0, 2)).reshape(RANGE, SNAP).astype(jnp.float32)
        weight_row = lax.dynamic_index_in_dim(training, bin_id, 0, keepdims=False).astype(jnp.float32)
        gram_matrix = jnp.dot((snapshot * weight_row[:, None]).T, snapshot, precision=highest)
        matrix = full_matrix(gram_matrix)
        weights = mvdr_weights(matrix[None], steer)[0]
        output = jnp.dot(weights.astype(jnp.float32).T, snapshot.T, precision=highest)
        return output.reshape(2, LOOKS, RANGE)
    return lax.map(one_bin, jnp.arange(DOPPLER, dtype=jnp.int32))
```

```python
import jax
import jax.numpy as jnp
from jax import lax
from jax.sharding import PartitionSpec as P

CH = 32
PULSES = 128
LOOKS = 64
ANGLES = 256
SNAP = 192


loading = 0.1
epsilon = 1e-06
block_pairs = ((0, 0), (0, 1), (0, 2), (1, 1), (1, 2), (2, 2))


def padded(block, sides, width):
    for axis, dim in sides:
        count = lax.axis_size(axis)
        forward = [(i, i + 1) for i in range(count - 1)]
        forward.append((count - 1, 0))
        backward = [(target, source) for source, target in forward]
        low = lax.ppermute(
            lax.slice_in_dim(block, block.shape[dim] - width, None, axis=dim), axis, forward
        )
        high = lax.ppermute(lax.slice_in_dim(block, 0, width, axis=dim), axis, backward)
        block = jnp.concatenate([low, block, high], axis=dim)
    return block


def split_up(array, dim, count):
    dims = array.shape
    blocks = array.reshape(*dims[:dim], count, dims[dim] // count, *dims[dim + 1 :])
    return jnp.moveaxis(blocks, dim, 0)


def sum_at_owner(array, axis, dim):
    blocks = split_up(array, dim, lax.axis_size(axis))
    arrived = lax.all_to_all(blocks, axis, split_axis=0, concat_axis=0, tiled=True)
    return arrived.sum(axis=0)


def in_order(blocks, dim):
    dims = list(blocks.shape[1:])
    dims[dim] *= blocks.shape[0]
    return jnp.moveaxis(blocks, 0, dim).reshape(dims)


def copy_for_each(array, axis):
    count = lax.axis_size(axis)
    return lax.all_to_all(
        jnp.broadcast_to(array[None], (count, *array.shape)), axis, 0, 0, tiled=True
    )


def gather_directly(array, axis, dim):
    return in_order(copy_for_each(array, axis), dim)


def twiddles():
    pulse_ids = jnp.arange(PULSES, dtype=jnp.int32)
    phase_ids = pulse_ids[:, None] * pulse_ids[None, :] % PULSES
    angles = phase_ids.astype(jnp.float32) * (2.0 * jnp.pi / PULSES)
    return jnp.concatenate([jnp.cos(angles), jnp.sin(angles)], axis=0).astype(jnp.bfloat16)


def doppler_spectra(echo_rows, twiddle):
    product = jnp.einsum("kp,rqcp->krqc", twiddle, echo_rows, preferred_element_type=jnp.float32)
    cosine = product[:PULSES]
    sine = product[PULSES:]
    real_part = cosine[:, :, 0] + sine[:, :, 1]
    imag_part = cosine[:, :, 1] - sine[:, :, 0]
    return (
        jnp.stack([real_part, imag_part], axis=2)
        .reshape(PULSES, echo_rows.shape[0], 2 * CH)
        .astype(jnp.bfloat16)
    )


def steering(look_index):
    sines = -1.0 + (2.0 * look_index.astype(jnp.float32) + 1.0) / ANGLES
    channel_ids = jnp.arange(CH).astype(jnp.float32)
    phases = jnp.pi * channel_ids[:, None] * sines[None, :]
    zeros = jnp.zeros((CH, LOOKS), jnp.float32)
    return jnp.stack([zeros, zeros, jnp.cos(phases), jnp.sin(phases), zeros, zeros]).reshape(
        SNAP, LOOKS
    )


def rotate(values):
    return jnp.concatenate([-values[..., CH:], values[..., :CH]], axis=-1)


def upper_blocks(edged, mask_rows):
    bin_count = edged.shape[0] - 2
    rotated = rotate(edged)
    snap = jnp.concatenate([edged[b : b + bin_count] for b in range(3)], axis=-1)
    turned_snap = jnp.concatenate([rotated[b : b + bin_count] for b in range(3)], axis=-1)
    both = jnp.concatenate([snap, turned_snap], axis=1)
    weighting = jnp.concatenate([mask_rows, mask_rows], axis=1)[:, :, None]
    masked = both * weighting
    pieces = []
    for left_pos in range(3):
        pieces.append(
            jnp.einsum(
                "krn,krm->knm",
                masked[:, :, left_pos * 2 * CH : left_pos * 2 * CH + CH],
                both[:, :, left_pos * 2 * CH :],
                preferred_element_type=jnp.float32,
            )
        )
    return jnp.concatenate(pieces, axis=-1)


def full_from_upper(upper):
    width = 2 * CH

    def block(left_pos, right_pos):
        if left_pos > right_pos:
            return jnp.swapaxes(block(right_pos, left_pos), 1, 2)
        start = block_pairs.index((left_pos, right_pos)) * width
        piece = upper[:, :, start : start + width]
        same, cross = piece[..., :CH], piece[..., CH:]
        return jnp.concatenate(
            [jnp.concatenate([same, cross], -1), jnp.concatenate([-cross, same], -1)], 1
        )

    rows = [jnp.concatenate([block(b, c) for c in range(3)], -1) for b in range(3)]
    return jnp.concatenate(rows, 1)


def unit_vectors(matrix, steer):
    bin_count = matrix.shape[0]
    power = jnp.trace(matrix, axis1=1, axis2=2) / SNAP + epsilon
    regular = matrix / power[:, None, None] + loading * jnp.eye(SNAP, dtype=jnp.float32)
    factor = jnp.linalg.cholesky(regular)
    targets = jnp.broadcast_to(steer, (bin_count, SNAP, LOOKS))
    forward = lax.linalg.triangular_solve(factor, targets, left_side=True, lower=True)
    solved = lax.linalg.triangular_solve(
        factor, forward, left_side=True, lower=True, transpose_a=True
    )
    gains = jnp.sum(targets * solved, axis=1)
    return (solved / jnp.sqrt(gains)[:, None, :]).astype(jnp.bfloat16)


def body(echoes, training, look_index):
    spectra = doppler_spectra(echoes, twiddles())
    turned = lax.all_to_all(spectra, "dop", split_axis=0, concat_axis=1, tiled=True)
    edged = padded(turned, (("dop", 0),), 1)
    bin_count = edged.shape[0] - 2
    upper = upper_blocks(edged, training.astype(jnp.bfloat16))
    my_upper = lax.psum_scatter(upper, "rng", scatter_dimension=0, tiled=True)
    my_unit = unit_vectors(full_from_upper(my_upper), steering(look_index))
    unit = lax.all_gather(my_unit, "rng", axis=0, tiled=True)
    shaped = unit.reshape(bin_count, 3, 2, CH, LOOKS)
    rotated = jnp.stack([-shaped[:, :, 1], shaped[:, :, 0]], axis=2).reshape(bin_count, SNAP, LOOKS)
    weights = jnp.concatenate([unit, rotated], axis=2)
    summed = None
    for position in range(3):
        term = jnp.einsum(
            "knj,krn->kjr",
            weights[:, position * 2 * CH : (position + 1) * 2 * CH],
            edged[position : position + bin_count],
            preferred_element_type=jnp.float32,
        )
        summed = term if summed is None else summed + term
    return summed.reshape(bin_count, 2, LOOKS, edged.shape[1])


def solution(mesh):
    in_specs = (P(("rng", "dop"), None, None, None), P("dop", "rng"), P())
    out_specs = P("dop", None, None, "rng")
    return jax.shard_map(body, mesh=mesh, in_specs=in_specs, out_specs=out_specs, check_vma=False)
```

```python
import jax
import jax.numpy as jnp
from jax import lax
from jax.sharding import PartitionSpec as P

CH = 32
PULSES = 128
LOOKS = 64
ANGLES = 256
SNAP = 192


loading = 0.1
epsilon = 1e-06
block_pairs = ((0, 0), (0, 1), (0, 2), (1, 1), (1, 2), (2, 2))


def padded(block, sides, width):
    for axis, dim in sides:
        count = lax.axis_size(axis)
        forward = [(i, i + 1) for i in range(count - 1)]
        forward.append((count - 1, 0))
        backward = [(target, source) for source, target in forward]
        low = lax.ppermute(
            lax.slice_in_dim(block, block.shape[dim] - width, None, axis=dim), axis, forward
        )
        high = lax.ppermute(lax.slice_in_dim(block, 0, width, axis=dim), axis, backward)
        block = jnp.concatenate([low, block, high], axis=dim)
    return block


def split_up(array, dim, count):
    dims = array.shape
    blocks = array.reshape(*dims[:dim], count, dims[dim] // count, *dims[dim + 1 :])
    return jnp.moveaxis(blocks, dim, 0)


def sum_at_owner(array, axis, dim):
    blocks = split_up(array, dim, lax.axis_size(axis))
    arrived = lax.all_to_all(blocks, axis, split_axis=0, concat_axis=0, tiled=True)
    return arrived.sum(axis=0)


def in_order(blocks, dim):
    dims = list(blocks.shape[1:])
    dims[dim] *= blocks.shape[0]
    return jnp.moveaxis(blocks, 0, dim).reshape(dims)


def copy_for_each(array, axis):
    count = lax.axis_size(axis)
    return lax.all_to_all(
        jnp.broadcast_to(array[None], (count, *array.shape)), axis, 0, 0, tiled=True
    )


def gather_directly(array, axis, dim):
    return in_order(copy_for_each(array, axis), dim)


def twiddles():
    pulse_ids = jnp.arange(PULSES, dtype=jnp.int32)
    phase_ids = pulse_ids[:, None] * pulse_ids[None, :] % PULSES
    angles = phase_ids.astype(jnp.float32) * (2.0 * jnp.pi / PULSES)
    return jnp.concatenate([jnp.cos(angles), jnp.sin(angles)], axis=0).astype(jnp.bfloat16)


def doppler_spectra(echo_rows, twiddle):
    product = jnp.einsum("kp,rqcp->krqc", twiddle, echo_rows, preferred_element_type=jnp.float32)
    cosine = product[:PULSES]
    sine = product[PULSES:]
    real_part = cosine[:, :, 0] + sine[:, :, 1]
    imag_part = cosine[:, :, 1] - sine[:, :, 0]
    return (
        jnp.stack([real_part, imag_part], axis=2)
        .reshape(PULSES, echo_rows.shape[0], 2 * CH)
        .astype(jnp.bfloat16)
    )


def steering(look_index):
    sines = -1.0 + (2.0 * look_index.astype(jnp.float32) + 1.0) / ANGLES
    channel_ids = jnp.arange(CH).astype(jnp.float32)
    phases = jnp.pi * channel_ids[:, None] * sines[None, :]
    zeros = jnp.zeros((CH, LOOKS), jnp.float32)
    return jnp.stack([zeros, zeros, jnp.cos(phases), jnp.sin(phases), zeros, zeros]).reshape(
        SNAP, LOOKS
    )


def rotate(values):
    return jnp.concatenate([-values[..., CH:], values[..., :CH]], axis=-1)


def upper_blocks(edged, mask_rows):
    bin_count = edged.shape[0] - 2
    rotated = rotate(edged)
    snap = jnp.concatenate([edged[b : b + bin_count] for b in range(3)], axis=-1)
    turned_snap = jnp.concatenate([rotated[b : b + bin_count] for b in range(3)], axis=-1)
    both = jnp.concatenate([snap, turned_snap], axis=1)
    weighting = jnp.concatenate([mask_rows, mask_rows], axis=1)[:, :, None]
    masked = both * weighting
    pieces = []
    for left_pos in range(3):
        pieces.append(
            jnp.einsum(
                "krn,krm->knm",
                masked[:, :, left_pos * 2 * CH : left_pos * 2 * CH + CH],
                both[:, :, left_pos * 2 * CH :],
                preferred_element_type=jnp.float32,
            )
        )
    return jnp.concatenate(pieces, axis=-1)


def full_from_upper(upper):
    width = 2 * CH

    def block(left_pos, right_pos):
        if left_pos > right_pos:
            return jnp.swapaxes(block(right_pos, left_pos), 1, 2)
        start = block_pairs.index((left_pos, right_pos)) * width
        piece = upper[:, :, start : start + width]
        same, cross = piece[..., :CH], piece[..., CH:]
        return jnp.concatenate(
            [jnp.concatenate([same, cross], -1), jnp.concatenate([-cross, same], -1)], 1
        )

    rows = [jnp.concatenate([block(b, c) for c in range(3)], -1) for b in range(3)]
    return jnp.concatenate(rows, 1)


def unit_vectors(matrix, steer):
    bin_count = matrix.shape[0]
    power = jnp.trace(matrix, axis1=1, axis2=2) / SNAP + epsilon
    regular = matrix / power[:, None, None] + loading * jnp.eye(SNAP, dtype=jnp.float32)
    factor = jnp.linalg.cholesky(regular)
    targets = jnp.broadcast_to(steer, (bin_count, SNAP, LOOKS))
    forward = lax.linalg.triangular_solve(factor, targets, left_side=True, lower=True)
    solved = lax.linalg.triangular_solve(
        factor, forward, left_side=True, lower=True, transpose_a=True
    )
    gains = jnp.sum(targets * solved, axis=1)
    return (solved / jnp.sqrt(gains)[:, None, :]).astype(jnp.bfloat16)


def body(echoes, training, look_index):
    spectra = doppler_spectra(echoes, twiddles())
    turned = lax.all_to_all(spectra, "dop", split_axis=0, concat_axis=1, tiled=True)
    edged = padded(turned, (("dop", 0),), 1)
    bin_count = edged.shape[0] - 2
    upper = upper_blocks(edged, training.astype(jnp.bfloat16))
    my_upper = sum_at_owner(upper, "rng", 0)
    my_unit = unit_vectors(full_from_upper(my_upper), steering(look_index))
    unit = gather_directly(my_unit, "rng", 0)
    shaped = unit.reshape(bin_count, 3, 2, CH, LOOKS)
    rotated = jnp.stack([-shaped[:, :, 1], shaped[:, :, 0]], axis=2).reshape(bin_count, SNAP, LOOKS)
    weights = jnp.concatenate([unit, rotated], axis=2)
    summed = None
    for position in range(3):
        term = jnp.einsum(
            "knj,krn->kjr",
            weights[:, position * 2 * CH : (position + 1) * 2 * CH],
            edged[position : position + bin_count],
            preferred_element_type=jnp.float32,
        )
        summed = term if summed is None else summed + term
    return summed.reshape(bin_count, 2, LOOKS, edged.shape[1])


def solution(mesh):
    in_specs = (P(("rng", "dop"), None, None, None), P("dop", "rng"), P())
    out_specs = P("dop", None, None, "rng")
    return jax.shard_map(body, mesh=mesh, in_specs=in_specs, out_specs=out_specs, check_vma=False)
```

```python
import jax
import jax.numpy as jnp
from jax import lax
from jax.sharding import PartitionSpec as P
from jax.experimental import pallas as pl
from jax.experimental.pallas import tpu as pltpu

CH = 32
PULSES = 128
LOOKS = 64
ANGLES = 256
SNAP = 192


loading = 0.1
epsilon = 1e-06
block_pairs = ((0, 0), (0, 1), (0, 2), (1, 1), (1, 2), (2, 2))


def padded(block, sides, width):
    for axis, dim in sides:
        count = lax.axis_size(axis)
        forward = [(i, i + 1) for i in range(count - 1)]
        forward.append((count - 1, 0))
        backward = [(target, source) for source, target in forward]
        low = lax.ppermute(
            lax.slice_in_dim(block, block.shape[dim] - width, None, axis=dim), axis, forward
        )
        high = lax.ppermute(lax.slice_in_dim(block, 0, width, axis=dim), axis, backward)
        block = jnp.concatenate([low, block, high], axis=dim)
    return block


def split_up(array, dim, count):
    dims = array.shape
    blocks = array.reshape(*dims[:dim], count, dims[dim] // count, *dims[dim + 1 :])
    return jnp.moveaxis(blocks, dim, 0)


def sum_at_owner(array, axis, dim):
    blocks = split_up(array, dim, lax.axis_size(axis))
    arrived = lax.all_to_all(blocks, axis, split_axis=0, concat_axis=0, tiled=True)
    return arrived.sum(axis=0)


def in_order(blocks, dim):
    dims = list(blocks.shape[1:])
    dims[dim] *= blocks.shape[0]
    return jnp.moveaxis(blocks, 0, dim).reshape(dims)


def copy_for_each(array, axis):
    count = lax.axis_size(axis)
    return lax.all_to_all(
        jnp.broadcast_to(array[None], (count, *array.shape)), axis, 0, 0, tiled=True
    )


def gather_directly(array, axis, dim):
    return in_order(copy_for_each(array, axis), dim)


def twiddles():
    pulse_ids = jnp.arange(PULSES, dtype=jnp.int32)
    phase_ids = pulse_ids[:, None] * pulse_ids[None, :] % PULSES
    angles = phase_ids.astype(jnp.float32) * (2.0 * jnp.pi / PULSES)
    return jnp.concatenate([jnp.cos(angles), jnp.sin(angles)], axis=0).astype(jnp.bfloat16)


def doppler_spectra(echo_rows, twiddle):
    product = jnp.einsum("kp,rqcp->krqc", twiddle, echo_rows, preferred_element_type=jnp.float32)
    cosine = product[:PULSES]
    sine = product[PULSES:]
    real_part = cosine[:, :, 0] + sine[:, :, 1]
    imag_part = cosine[:, :, 1] - sine[:, :, 0]
    return (
        jnp.stack([real_part, imag_part], axis=2)
        .reshape(PULSES, echo_rows.shape[0], 2 * CH)
        .astype(jnp.bfloat16)
    )


def steering(look_index):
    sines = -1.0 + (2.0 * look_index.astype(jnp.float32) + 1.0) / ANGLES
    channel_ids = jnp.arange(CH).astype(jnp.float32)
    phases = jnp.pi * channel_ids[:, None] * sines[None, :]
    zeros = jnp.zeros((CH, LOOKS), jnp.float32)
    return jnp.stack([zeros, zeros, jnp.cos(phases), jnp.sin(phases), zeros, zeros]).reshape(
        SNAP, LOOKS
    )


def rotate(values):
    return jnp.concatenate([-values[..., CH:], values[..., :CH]], axis=-1)


def upper_blocks(edged, mask_rows):
    bin_count = edged.shape[0] - 2
    rotated = rotate(edged)
    snap = jnp.concatenate([edged[b : b + bin_count] for b in range(3)], axis=-1)
    turned_snap = jnp.concatenate([rotated[b : b + bin_count] for b in range(3)], axis=-1)
    both = jnp.concatenate([snap, turned_snap], axis=1)
    weighting = jnp.concatenate([mask_rows, mask_rows], axis=1)[:, :, None]
    masked = both * weighting
    pieces = []
    for left_pos in range(3):
        pieces.append(
            jnp.einsum(
                "krn,krm->knm",
                masked[:, :, left_pos * 2 * CH : left_pos * 2 * CH + CH],
                both[:, :, left_pos * 2 * CH :],
                preferred_element_type=jnp.float32,
            )
        )
    return jnp.concatenate(pieces, axis=-1)


def full_from_upper(upper):
    width = 2 * CH

    def block(left_pos, right_pos):
        if left_pos > right_pos:
            return jnp.swapaxes(block(right_pos, left_pos), 1, 2)
        start = block_pairs.index((left_pos, right_pos)) * width
        piece = upper[:, :, start : start + width]
        same, cross = piece[..., :CH], piece[..., CH:]
        return jnp.concatenate(
            [jnp.concatenate([same, cross], -1), jnp.concatenate([-cross, same], -1)], 1
        )

    rows = [jnp.concatenate([block(b, c) for c in range(3)], -1) for b in range(3)]
    return jnp.concatenate(rows, 1)


def eliminate(aug_ref, out_ref, work_ref):
    rows, cols = work_ref.shape
    work_ref[...] = aug_ref[0]
    lane_ids = lax.broadcasted_iota(jnp.int32, (1, cols), 1)
    row_ids = lax.broadcasted_iota(jnp.int32, (rows, 1), 0)

    def step(j, carry):
        current = work_ref[...]
        pivot_row = work_ref[pl.ds(j, 1), :]
        lane_hit = lane_ids == j
        column = jnp.sum(jnp.where(lane_hit, current, 0.0), axis=1, keepdims=True)
        pivot = jnp.sum(jnp.where(lane_hit, pivot_row, 0.0), axis=1, keepdims=True)
        scaled = pivot_row / pivot
        work_ref[...] = jnp.where(row_ids == j, scaled, current - column * scaled)
        return carry

    lax.fori_loop(0, rows, step, 0)
    out_ref[0] = work_ref[...]


def solve_systems(matrix, targets):
    count, size, _ = matrix.shape
    aug = jnp.concatenate([matrix, targets], axis=2)
    spec = pl.BlockSpec((1, size, aug.shape[2]), lambda i: (i, 0, 0))
    out = pl.pallas_call(
        eliminate,
        grid=(count,),
        in_specs=[spec],
        out_specs=spec,
        out_shape=jax.ShapeDtypeStruct(aug.shape, jnp.float32),
        scratch_shapes=[pltpu.VMEM((size, aug.shape[2]), jnp.float32)],
    )(aug)
    return out[:, :, size:]


def unit_vectors(matrix, steer):
    bin_count = matrix.shape[0]
    power = jnp.trace(matrix, axis1=1, axis2=2) / SNAP + epsilon
    regular = matrix / power[:, None, None] + loading * jnp.eye(SNAP, dtype=jnp.float32)
    targets = jnp.broadcast_to(steer, (bin_count, SNAP, LOOKS))
    solved = solve_systems(regular, targets)
    gains = jnp.sum(targets * solved, axis=1)
    return (solved / jnp.sqrt(gains)[:, None, :]).astype(jnp.bfloat16)


def body(echoes, training, look_index):
    spectra = doppler_spectra(echoes, twiddles())
    turned = lax.all_to_all(spectra, "dop", split_axis=0, concat_axis=1, tiled=True)
    edged = padded(turned, (("dop", 0),), 1)
    bin_count = edged.shape[0] - 2
    upper = upper_blocks(edged, training.astype(jnp.bfloat16))
    my_upper = sum_at_owner(upper, "rng", 0)
    my_unit = unit_vectors(full_from_upper(my_upper), steering(look_index))
    unit = gather_directly(my_unit, "rng", 0)
    shaped = unit.reshape(bin_count, 3, 2, CH, LOOKS)
    rotated = jnp.stack([-shaped[:, :, 1], shaped[:, :, 0]], axis=2).reshape(bin_count, SNAP, LOOKS)
    weights = jnp.concatenate([unit, rotated], axis=2)
    summed = None
    for position in range(3):
        term = jnp.einsum(
            "knj,krn->kjr",
            weights[:, position * 2 * CH : (position + 1) * 2 * CH],
            edged[position : position + bin_count],
            preferred_element_type=jnp.float32,
        )
        summed = term if summed is None else summed + term
    return summed.reshape(bin_count, 2, LOOKS, edged.shape[1])


def solution(mesh):
    in_specs = (P(("rng", "dop"), None, None, None), P("dop", "rng"), P())
    out_specs = P("dop", None, None, "rng")
    return jax.shard_map(body, mesh=mesh, in_specs=in_specs, out_specs=out_specs, check_vma=False)
```

```python
import jax
import jax.numpy as jnp
from jax import lax
from jax.sharding import PartitionSpec as P
from jax.experimental import pallas as pl
from jax.experimental.pallas import tpu as pltpu

CH = 32
PULSES = 128
LOOKS = 64
ANGLES = 256
SNAP = 192


loading = 0.1
epsilon = 1e-06
block_pairs = ((0, 0), (0, 1), (0, 2), (1, 1), (1, 2), (2, 2))


def padded(block, sides, width):
    for axis, dim in sides:
        count = lax.axis_size(axis)
        forward = [(i, i + 1) for i in range(count - 1)]
        forward.append((count - 1, 0))
        backward = [(target, source) for source, target in forward]
        low = lax.ppermute(
            lax.slice_in_dim(block, block.shape[dim] - width, None, axis=dim), axis, forward
        )
        high = lax.ppermute(lax.slice_in_dim(block, 0, width, axis=dim), axis, backward)
        block = jnp.concatenate([low, block, high], axis=dim)
    return block


def split_up(array, dim, count):
    dims = array.shape
    blocks = array.reshape(*dims[:dim], count, dims[dim] // count, *dims[dim + 1 :])
    return jnp.moveaxis(blocks, dim, 0)


def sum_at_owner(array, axis, dim):
    blocks = split_up(array, dim, lax.axis_size(axis))
    arrived = lax.all_to_all(blocks, axis, split_axis=0, concat_axis=0, tiled=True)
    return arrived.sum(axis=0)


def in_order(blocks, dim):
    dims = list(blocks.shape[1:])
    dims[dim] *= blocks.shape[0]
    return jnp.moveaxis(blocks, 0, dim).reshape(dims)


def copy_for_each(array, axis):
    count = lax.axis_size(axis)
    return lax.all_to_all(
        jnp.broadcast_to(array[None], (count, *array.shape)), axis, 0, 0, tiled=True
    )


def gather_directly(array, axis, dim):
    return in_order(copy_for_each(array, axis), dim)


def twiddles(bin_ids):
    pulse_ids = jnp.arange(PULSES, dtype=jnp.int32)
    phase_ids = bin_ids[:, None] * pulse_ids[None, :] % PULSES
    angles = phase_ids.astype(jnp.float32) * (2.0 * jnp.pi / PULSES)
    return jnp.concatenate([jnp.cos(angles), jnp.sin(angles)], axis=0).astype(jnp.bfloat16)


def doppler_spectra(echo_rows, twiddle):
    product = jnp.einsum("kp,rqcp->krqc", twiddle, echo_rows, preferred_element_type=jnp.float32)
    half = twiddle.shape[0] // 2
    cosine = product[:half]
    sine = product[half:]
    real_part = cosine[:, :, 0] + sine[:, :, 1]
    imag_part = cosine[:, :, 1] - sine[:, :, 0]
    return (
        jnp.stack([real_part, imag_part], axis=2)
        .reshape(half, echo_rows.shape[0], 2 * CH)
        .astype(jnp.bfloat16)
    )


def steering(look_index):
    sines = -1.0 + (2.0 * look_index.astype(jnp.float32) + 1.0) / ANGLES
    channel_ids = jnp.arange(CH).astype(jnp.float32)
    phases = jnp.pi * channel_ids[:, None] * sines[None, :]
    zeros = jnp.zeros((CH, LOOKS), jnp.float32)
    return jnp.stack([zeros, zeros, jnp.cos(phases), jnp.sin(phases), zeros, zeros]).reshape(
        SNAP, LOOKS
    )


def rotate(values):
    return jnp.concatenate([-values[..., CH:], values[..., :CH]], axis=-1)


def upper_blocks(edged, mask_rows):
    bin_count = edged.shape[0] - 2
    rotated = rotate(edged)
    snap = jnp.concatenate([edged[b : b + bin_count] for b in range(3)], axis=-1)
    turned_snap = jnp.concatenate([rotated[b : b + bin_count] for b in range(3)], axis=-1)
    both = jnp.concatenate([snap, turned_snap], axis=1)
    weighting = jnp.concatenate([mask_rows, mask_rows], axis=1)[:, :, None]
    masked = both * weighting
    pieces = []
    for left_pos in range(3):
        pieces.append(
            jnp.einsum(
                "krn,krm->knm",
                masked[:, :, left_pos * 2 * CH : left_pos * 2 * CH + CH],
                both[:, :, left_pos * 2 * CH :],
                preferred_element_type=jnp.float32,
            )
        )
    return snap, jnp.concatenate(pieces, axis=-1)


def full_from_upper(upper):
    width = 2 * CH

    def block(left_pos, right_pos):
        if left_pos > right_pos:
            return jnp.swapaxes(block(right_pos, left_pos), 1, 2)
        start = block_pairs.index((left_pos, right_pos)) * width
        piece = upper[:, :, start : start + width]
        same, cross = piece[..., :CH], piece[..., CH:]
        return jnp.concatenate(
            [jnp.concatenate([same, cross], -1), jnp.concatenate([-cross, same], -1)], 1
        )

    rows = [jnp.concatenate([block(b, c) for c in range(3)], -1) for b in range(3)]
    return jnp.concatenate(rows, 1)


def eliminate(aug_ref, out_ref, work_ref):
    rows, cols = work_ref.shape
    work_ref[...] = aug_ref[0]
    lane_ids = lax.broadcasted_iota(jnp.int32, (1, cols), 1)
    row_ids = lax.broadcasted_iota(jnp.int32, (rows, 1), 0)

    def step(j, carry):
        current = work_ref[...]
        pivot_row = work_ref[pl.ds(j, 1), :]
        lane_hit = lane_ids == j
        column = jnp.sum(jnp.where(lane_hit, current, 0.0), axis=1, keepdims=True)
        pivot = jnp.sum(jnp.where(lane_hit, pivot_row, 0.0), axis=1, keepdims=True)
        scaled = pivot_row / pivot
        work_ref[...] = jnp.where(row_ids == j, scaled, current - column * scaled)
        return carry

    lax.fori_loop(0, rows, step, 0)
    out_ref[0] = work_ref[...]


def solve_systems(matrix, targets):
    count, size, _ = matrix.shape
    aug = jnp.concatenate([matrix, targets], axis=2)
    spec = pl.BlockSpec((1, size, aug.shape[2]), lambda i: (i, 0, 0))
    out = pl.pallas_call(
        eliminate,
        grid=(count,),
        in_specs=[spec],
        out_specs=spec,
        out_shape=jax.ShapeDtypeStruct(aug.shape, jnp.float32),
        scratch_shapes=[pltpu.VMEM((size, aug.shape[2]), jnp.float32)],
    )(aug)
    return out[:, :, size:]


def unit_vectors(matrix, steer):
    bin_count = matrix.shape[0]
    power = jnp.trace(matrix, axis1=1, axis2=2) / SNAP + epsilon
    regular = matrix / power[:, None, None] + loading * jnp.eye(SNAP, dtype=jnp.float32)
    targets = jnp.broadcast_to(steer, (bin_count, SNAP, LOOKS))
    solved = solve_systems(regular, targets)
    gains = jnp.sum(targets * solved, axis=1)
    return (solved / jnp.sqrt(gains)[:, None, :]).astype(jnp.bfloat16)


def body(echoes, training, look_index):
    groups = lax.axis_size("dop")
    bins_here = PULSES // groups
    wanted = (jnp.arange(groups)[:, None] * bins_here + jnp.arange(bins_here + 2)[None, :] - 1) % PULSES
    spectra = doppler_spectra(echoes, twiddles(wanted.reshape(-1).astype(jnp.int32)))
    sent = spectra.reshape(groups, bins_here + 2, echoes.shape[0], 2 * CH)
    arrived = lax.all_to_all(sent, "dop", 0, 0)
    edged = jnp.moveaxis(arrived, 0, 1).reshape(bins_here + 2, groups * echoes.shape[0], 2 * CH)
    bin_count = bins_here
    snap, upper = upper_blocks(edged, training.astype(jnp.bfloat16))
    my_upper = sum_at_owner(upper, "rng", 0)
    my_unit = unit_vectors(full_from_upper(my_upper), steering(look_index))
    unit = gather_directly(my_unit, "rng", 0)
    shaped = unit.reshape(bin_count, 3, 2, CH, LOOKS)
    rotated = jnp.stack([-shaped[:, :, 1], shaped[:, :, 0]], axis=2).reshape(bin_count, SNAP, LOOKS)
    weights = jnp.concatenate([unit, rotated], axis=2)
    summed = jnp.einsum("knj,krn->kjr", weights, snap, preferred_element_type=jnp.float32)
    return summed.reshape(bin_count, 2, LOOKS, edged.shape[1])


def solution(mesh):
    in_specs = (P(("rng", "dop"), None, None, None), P("dop", "rng"), P())
    out_specs = P("dop", None, None, "rng")
    return jax.shard_map(body, mesh=mesh, in_specs=in_specs, out_specs=out_specs, check_vma=False)
```

```python
import jax
import jax.numpy as jnp
from jax import lax
from jax.sharding import PartitionSpec as P
from jax.experimental import pallas as pl
from jax.experimental.pallas import tpu as pltpu

CH = 32
PULSES = 128
LOOKS = 64
ANGLES = 256
SNAP = 192


loading = 0.1
epsilon = 1e-06
block_pairs = ((0, 0), (0, 1), (0, 2), (1, 1), (1, 2), (2, 2))


def padded(block, sides, width):
    for axis, dim in sides:
        count = lax.axis_size(axis)
        forward = [(i, i + 1) for i in range(count - 1)]
        forward.append((count - 1, 0))
        backward = [(target, source) for source, target in forward]
        low = lax.ppermute(
            lax.slice_in_dim(block, block.shape[dim] - width, None, axis=dim), axis, forward
        )
        high = lax.ppermute(lax.slice_in_dim(block, 0, width, axis=dim), axis, backward)
        block = jnp.concatenate([low, block, high], axis=dim)
    return block


def split_up(array, dim, count):
    dims = array.shape
    blocks = array.reshape(*dims[:dim], count, dims[dim] // count, *dims[dim + 1 :])
    return jnp.moveaxis(blocks, dim, 0)


def sum_at_owner(array, axis, dim):
    blocks = split_up(array, dim, lax.axis_size(axis))
    arrived = lax.all_to_all(blocks, axis, split_axis=0, concat_axis=0, tiled=True)
    return arrived.sum(axis=0)


def in_order(blocks, dim):
    dims = list(blocks.shape[1:])
    dims[dim] *= blocks.shape[0]
    return jnp.moveaxis(blocks, 0, dim).reshape(dims)


def copy_for_each(array, axis):
    count = lax.axis_size(axis)
    return lax.all_to_all(
        jnp.broadcast_to(array[None], (count, *array.shape)), axis, 0, 0, tiled=True
    )


def gather_directly(array, axis, dim):
    return in_order(copy_for_each(array, axis), dim)


def ring_groups(count, inner):
    outer = count // inner
    along_inner = [[o * inner + i for i in range(inner)] for o in range(outer)]
    along_outer = [[o * inner + i for o in range(outer)] for i in range(inner)]
    return along_inner, along_outer


def sum_in_stages(array, axis, inner):
    count = lax.axis_size(axis)
    outer = count // inner
    along_inner, along_outer = ring_groups(count, inner)
    blocks = array.reshape(outer, inner, array.shape[0] // count, *array.shape[1:])
    first = lax.all_to_all(blocks, axis, 1, 1, axis_index_groups=along_inner).sum(axis=1)
    second = lax.all_to_all(first, axis, 0, 0, axis_index_groups=along_outer).sum(axis=0)
    return second


def gather_in_stages(array, axis, inner):
    count = lax.axis_size(axis)
    outer = count // inner
    along_inner, along_outer = ring_groups(count, inner)
    first = lax.all_to_all(
        jnp.broadcast_to(array[None], (outer, *array.shape)), axis, 0, 0,
        axis_index_groups=along_outer,
    )
    second = lax.all_to_all(
        jnp.broadcast_to(first[None], (inner, *first.shape)), axis, 0, 0,
        axis_index_groups=along_inner,
    )
    return jnp.swapaxes(second, 0, 1).reshape(count * array.shape[0], *array.shape[1:])


def twiddles():
    pulse_ids = jnp.arange(PULSES, dtype=jnp.int32)
    phase_ids = pulse_ids[:, None] * pulse_ids[None, :] % PULSES
    angles = phase_ids.astype(jnp.float32) * (2.0 * jnp.pi / PULSES)
    return jnp.concatenate([jnp.cos(angles), jnp.sin(angles)], axis=0).astype(jnp.bfloat16)


def doppler_spectra(echo_rows, twiddle):
    product = jnp.einsum("kp,rqcp->krqc", twiddle, echo_rows, preferred_element_type=jnp.float32)
    cosine = product[:PULSES]
    sine = product[PULSES:]
    real_part = cosine[:, :, 0] + sine[:, :, 1]
    imag_part = cosine[:, :, 1] - sine[:, :, 0]
    return (
        jnp.stack([real_part, imag_part], axis=2)
        .reshape(PULSES, echo_rows.shape[0], 2 * CH)
        .astype(jnp.bfloat16)
    )


def steering(look_index):
    sines = -1.0 + (2.0 * look_index.astype(jnp.float32) + 1.0) / ANGLES
    channel_ids = jnp.arange(CH).astype(jnp.float32)
    phases = jnp.pi * channel_ids[:, None] * sines[None, :]
    zeros = jnp.zeros((CH, LOOKS), jnp.float32)
    return jnp.stack([zeros, zeros, jnp.cos(phases), jnp.sin(phases), zeros, zeros]).reshape(
        SNAP, LOOKS
    )


def rotate(values):
    return jnp.concatenate([-values[..., CH:], values[..., :CH]], axis=-1)


def upper_blocks(edged, mask_rows):
    bin_count = edged.shape[0] - 2
    rotated = rotate(edged)
    snap = jnp.concatenate([edged[b : b + bin_count] for b in range(3)], axis=-1)
    turned_snap = jnp.concatenate([rotated[b : b + bin_count] for b in range(3)], axis=-1)
    both = jnp.concatenate([snap, turned_snap], axis=1)
    weighting = jnp.concatenate([mask_rows, mask_rows], axis=1)[:, :, None]
    masked = both * weighting
    pieces = []
    for left_pos in range(3):
        pieces.append(
            jnp.einsum(
                "krn,krm->knm",
                masked[:, :, left_pos * 2 * CH : left_pos * 2 * CH + CH],
                both[:, :, left_pos * 2 * CH :],
                preferred_element_type=jnp.float32,
            )
        )
    return jnp.concatenate(pieces, axis=-1)


def full_from_upper(upper):
    width = 2 * CH

    def block(left_pos, right_pos):
        if left_pos > right_pos:
            return jnp.swapaxes(block(right_pos, left_pos), 1, 2)
        start = block_pairs.index((left_pos, right_pos)) * width
        piece = upper[:, :, start : start + width]
        same, cross = piece[..., :CH], piece[..., CH:]
        return jnp.concatenate(
            [jnp.concatenate([same, cross], -1), jnp.concatenate([-cross, same], -1)], 1
        )

    rows = [jnp.concatenate([block(b, c) for c in range(3)], -1) for b in range(3)]
    return jnp.concatenate(rows, 1)


def eliminate(aug_ref, out_ref, work_ref):
    rows, cols = work_ref.shape
    work_ref[...] = aug_ref[0]
    lane_ids = lax.broadcasted_iota(jnp.int32, (1, cols), 1)
    row_ids = lax.broadcasted_iota(jnp.int32, (rows, 1), 0)

    def step(j, carry):
        current = work_ref[...]
        pivot_row = work_ref[pl.ds(j, 1), :]
        lane_hit = lane_ids == j
        column = jnp.sum(jnp.where(lane_hit, current, 0.0), axis=1, keepdims=True)
        pivot = jnp.sum(jnp.where(lane_hit, pivot_row, 0.0), axis=1, keepdims=True)
        scaled = pivot_row / pivot
        work_ref[...] = jnp.where(row_ids == j, scaled, current - column * scaled)
        return carry

    lax.fori_loop(0, rows, step, 0)
    out_ref[0] = work_ref[...]


def solve_systems(matrix, targets):
    count, size, _ = matrix.shape
    aug = jnp.concatenate([matrix, targets], axis=2)
    spec = pl.BlockSpec((1, size, aug.shape[2]), lambda i: (i, 0, 0))
    out = pl.pallas_call(
        eliminate,
        grid=(count,),
        in_specs=[spec],
        out_specs=spec,
        out_shape=jax.ShapeDtypeStruct(aug.shape, jnp.float32),
        scratch_shapes=[pltpu.VMEM((size, aug.shape[2]), jnp.float32)],
    )(aug)
    return out[:, :, size:]


def unit_vectors(matrix, steer):
    bin_count = matrix.shape[0]
    power = jnp.trace(matrix, axis1=1, axis2=2) / SNAP + epsilon
    regular = matrix / power[:, None, None] + loading * jnp.eye(SNAP, dtype=jnp.float32)
    targets = jnp.broadcast_to(steer, (bin_count, SNAP, LOOKS))
    solved = solve_systems(regular, targets)
    gains = jnp.sum(targets * solved, axis=1)
    return (solved / jnp.sqrt(gains)[:, None, :]).astype(jnp.bfloat16)


def body(echoes, training, look_index):
    spectra = doppler_spectra(echoes, twiddles())
    turned = lax.all_to_all(spectra, "dop", split_axis=0, concat_axis=1, tiled=True)
    edged = padded(turned, (("dop", 0),), 1)
    bin_count = edged.shape[0] - 2
    upper = upper_blocks(edged, training.astype(jnp.bfloat16))
    my_upper = sum_in_stages(upper, "rng", 4)
    my_unit = unit_vectors(full_from_upper(my_upper), steering(look_index))
    unit = gather_in_stages(my_unit, "rng", 4)
    shaped = unit.reshape(bin_count, 3, 2, CH, LOOKS)
    rotated = jnp.stack([-shaped[:, :, 1], shaped[:, :, 0]], axis=2).reshape(bin_count, SNAP, LOOKS)
    weights = jnp.concatenate([unit, rotated], axis=2)
    summed = None
    for position in range(3):
        term = jnp.einsum(
            "knj,krn->kjr",
            weights[:, position * 2 * CH : (position + 1) * 2 * CH],
            edged[position : position + bin_count],
            preferred_element_type=jnp.float32,
        )
        summed = term if summed is None else summed + term
    return summed.reshape(bin_count, 2, LOOKS, edged.shape[1])


def solution(mesh):
    in_specs = (P(("rng", "dop"), None, None, None), P("dop", "rng"), P())
    out_specs = P("dop", None, None, "rng")
    return jax.shard_map(body, mesh=mesh, in_specs=in_specs, out_specs=out_specs, check_vma=False)
```

```python
import jax
import jax.numpy as jnp
from jax import lax
from jax.sharding import PartitionSpec as P
from jax.experimental import pallas as pl
from jax.experimental.pallas import tpu as pltpu

CH = 32
PULSES = 128
LOOKS = 64
ANGLES = 256
SNAP = 192


loading = 0.1
epsilon = 1e-06
block_pairs = ((0, 0), (0, 1), (0, 2), (1, 1), (1, 2), (2, 2))


def padded(block, sides, width):
    for axis, dim in sides:
        count = lax.axis_size(axis)
        forward = [(i, i + 1) for i in range(count - 1)]
        forward.append((count - 1, 0))
        backward = [(target, source) for source, target in forward]
        low = lax.ppermute(
            lax.slice_in_dim(block, block.shape[dim] - width, None, axis=dim), axis, forward
        )
        high = lax.ppermute(lax.slice_in_dim(block, 0, width, axis=dim), axis, backward)
        block = jnp.concatenate([low, block, high], axis=dim)
    return block


def split_up(array, dim, count):
    dims = array.shape
    blocks = array.reshape(*dims[:dim], count, dims[dim] // count, *dims[dim + 1 :])
    return jnp.moveaxis(blocks, dim, 0)


def sum_at_owner(array, axis, dim):
    blocks = split_up(array, dim, lax.axis_size(axis))
    arrived = lax.all_to_all(blocks, axis, split_axis=0, concat_axis=0, tiled=True)
    return arrived.sum(axis=0)


def in_order(blocks, dim):
    dims = list(blocks.shape[1:])
    dims[dim] *= blocks.shape[0]
    return jnp.moveaxis(blocks, 0, dim).reshape(dims)


def copy_for_each(array, axis):
    count = lax.axis_size(axis)
    return lax.all_to_all(
        jnp.broadcast_to(array[None], (count, *array.shape)), axis, 0, 0, tiled=True
    )


def gather_directly(array, axis, dim):
    return in_order(copy_for_each(array, axis), dim)


def twiddles(bin_ids):
    pulse_ids = jnp.arange(PULSES, dtype=jnp.int32)
    phase_ids = bin_ids[:, None] * pulse_ids[None, :] % PULSES
    angles = phase_ids.astype(jnp.float32) * (2.0 * jnp.pi / PULSES)
    return jnp.concatenate([jnp.cos(angles), jnp.sin(angles)], axis=0).astype(jnp.bfloat16)


def doppler_spectra(echo_rows, twiddle):
    product = jnp.einsum("kp,rqcp->krqc", twiddle, echo_rows, preferred_element_type=jnp.float32)
    half = twiddle.shape[0] // 2
    cosine = product[:half]
    sine = product[half:]
    real_part = cosine[:, :, 0] + sine[:, :, 1]
    imag_part = cosine[:, :, 1] - sine[:, :, 0]
    return (
        jnp.stack([real_part, imag_part], axis=2)
        .reshape(half, echo_rows.shape[0], 2 * CH)
        .astype(jnp.bfloat16)
    )


def steering(look_index):
    sines = -1.0 + (2.0 * look_index.astype(jnp.float32) + 1.0) / ANGLES
    channel_ids = jnp.arange(CH).astype(jnp.float32)
    phases = jnp.pi * channel_ids[:, None] * sines[None, :]
    zeros = jnp.zeros((CH, LOOKS), jnp.float32)
    return jnp.stack([zeros, zeros, jnp.cos(phases), jnp.sin(phases), zeros, zeros]).reshape(
        SNAP, LOOKS
    )


def rotate(values):
    return jnp.concatenate([-values[..., CH:], values[..., :CH]], axis=-1)


def upper_blocks(edged, mask_rows):
    bin_count = edged.shape[0] - 2
    rotated = rotate(edged)
    snap = jnp.concatenate([edged[b : b + bin_count] for b in range(3)], axis=-1)
    turned_snap = jnp.concatenate([rotated[b : b + bin_count] for b in range(3)], axis=-1)
    both = jnp.concatenate([snap, turned_snap], axis=1)
    weighting = jnp.concatenate([mask_rows, mask_rows], axis=1)[:, :, None]
    masked = both * weighting
    pieces = []
    for left_pos in range(3):
        pieces.append(
            jnp.einsum(
                "krn,krm->knm",
                masked[:, :, left_pos * 2 * CH : left_pos * 2 * CH + CH],
                both[:, :, left_pos * 2 * CH :],
                preferred_element_type=jnp.float32,
            )
        )
    return jnp.concatenate(pieces, axis=-1)


def full_from_upper(upper):
    width = 2 * CH

    def block(left_pos, right_pos):
        if left_pos > right_pos:
            return jnp.swapaxes(block(right_pos, left_pos), 1, 2)
        start = block_pairs.index((left_pos, right_pos)) * width
        piece = upper[:, :, start : start + width]
        same, cross = piece[..., :CH], piece[..., CH:]
        return jnp.concatenate(
            [jnp.concatenate([same, cross], -1), jnp.concatenate([-cross, same], -1)], 1
        )

    rows = [jnp.concatenate([block(b, c) for c in range(3)], -1) for b in range(3)]
    return jnp.concatenate(rows, 1)


def eliminate(matrix_ref, steer_ref, unit_ref, work_ref):
    rows, cols = work_ref.shape
    matrix = matrix_ref[0]
    steer = steer_ref[...]
    lane_ids = lax.broadcasted_iota(jnp.int32, (1, cols), 1)
    row_ids = lax.broadcasted_iota(jnp.int32, (rows, 1), 0)
    diagonal = row_ids == lane_ids[:, :rows]
    power = jnp.sum(jnp.where(diagonal, matrix, 0.0)) / SNAP + epsilon
    work_ref[:, :rows] = matrix / power + jnp.where(diagonal, loading, 0.0)
    work_ref[:, rows:] = steer

    def step(j, carry):
        current = work_ref[...]
        pivot_row = work_ref[pl.ds(j, 1), :]
        lane_hit = lane_ids == j
        column = jnp.sum(jnp.where(lane_hit, current, 0.0), axis=1, keepdims=True)
        pivot = jnp.sum(jnp.where(lane_hit, pivot_row, 0.0), axis=1, keepdims=True)
        scaled = pivot_row / pivot
        work_ref[...] = jnp.where(row_ids == j, scaled, current - column * scaled)
        return carry

    lax.fori_loop(0, rows, step, 0)
    solved = work_ref[:, rows:]
    gains = jnp.sum(steer * solved, axis=0, keepdims=True)
    unit_ref[0] = (solved / jnp.sqrt(gains)).astype(unit_ref.dtype)


def unit_vectors(matrix, steer):
    count, size, _ = matrix.shape
    return pl.pallas_call(
        eliminate,
        grid=(count,),
        in_specs=[
            pl.BlockSpec((1, size, size), lambda i: (i, 0, 0)),
            pl.BlockSpec((size, LOOKS), lambda i: (0, 0)),
        ],
        out_specs=pl.BlockSpec((1, size, LOOKS), lambda i: (i, 0, 0)),
        out_shape=jax.ShapeDtypeStruct((count, size, LOOKS), jnp.bfloat16),
        scratch_shapes=[pltpu.VMEM((size, size + LOOKS), jnp.float32)],
    )(matrix, steer)


def body(echoes, training, look_index):
    groups = lax.axis_size("dop")
    bins_here = PULSES // groups
    wanted = (jnp.arange(groups)[:, None] * bins_here + jnp.arange(bins_here + 2)[None, :] - 1) % PULSES
    spectra = doppler_spectra(echoes, twiddles(wanted.reshape(-1).astype(jnp.int32)))
    edged = lax.all_to_all(spectra, "dop", split_axis=0, concat_axis=1, tiled=True)
    bin_count = bins_here
    upper = upper_blocks(edged, training.astype(jnp.bfloat16))
    my_upper = sum_at_owner(upper, "rng", 0)
    my_unit = unit_vectors(full_from_upper(my_upper), steering(look_index))
    unit = gather_directly(my_unit, "rng", 0)
    shaped = unit.reshape(bin_count, 3, 2, CH, LOOKS)
    rotated = jnp.stack([-shaped[:, :, 1], shaped[:, :, 0]], axis=2).reshape(bin_count, SNAP, LOOKS)
    weights = jnp.concatenate([unit, rotated], axis=2)
    summed = None
    for position in range(3):
        term = jnp.einsum(
            "knj,krn->kjr",
            weights[:, position * 2 * CH : (position + 1) * 2 * CH],
            edged[position : position + bin_count],
            preferred_element_type=jnp.float32,
        )
        summed = term if summed is None else summed + term
    return summed.reshape(bin_count, 2, LOOKS, edged.shape[1])


def solution(mesh):
    in_specs = (P(("rng", "dop"), None, None, None), P("dop", "rng"), P())
    out_specs = P("dop", None, None, "rng")
    return jax.shard_map(body, mesh=mesh, in_specs=in_specs, out_specs=out_specs, check_vma=False)
```

```python
import jax
import jax.numpy as jnp
from jax import lax
from jax.sharding import PartitionSpec as P
from jax.experimental import pallas as pl
from jax.experimental.pallas import tpu as pltpu

CH = 32
PULSES = 128
LOOKS = 64
ANGLES = 256
SNAP = 192


loading = 0.1
epsilon = 1e-06
block_pairs = ((0, 0), (0, 1), (0, 2), (1, 1), (1, 2), (2, 2))


def padded(block, sides, width):
    for axis, dim in sides:
        count = lax.axis_size(axis)
        forward = [(i, i + 1) for i in range(count - 1)]
        forward.append((count - 1, 0))
        backward = [(target, source) for source, target in forward]
        low = lax.ppermute(
            lax.slice_in_dim(block, block.shape[dim] - width, None, axis=dim), axis, forward
        )
        high = lax.ppermute(lax.slice_in_dim(block, 0, width, axis=dim), axis, backward)
        block = jnp.concatenate([low, block, high], axis=dim)
    return block


def split_up(array, dim, count):
    dims = array.shape
    blocks = array.reshape(*dims[:dim], count, dims[dim] // count, *dims[dim + 1 :])
    return jnp.moveaxis(blocks, dim, 0)


def sum_at_owner(array, axis, dim):
    blocks = split_up(array, dim, lax.axis_size(axis))
    arrived = lax.all_to_all(blocks, axis, split_axis=0, concat_axis=0, tiled=True)
    return arrived.sum(axis=0)


def in_order(blocks, dim):
    dims = list(blocks.shape[1:])
    dims[dim] *= blocks.shape[0]
    return jnp.moveaxis(blocks, 0, dim).reshape(dims)


def copy_for_each(array, axis):
    count = lax.axis_size(axis)
    return lax.all_to_all(
        jnp.broadcast_to(array[None], (count, *array.shape)), axis, 0, 0, tiled=True
    )


def gather_directly(array, axis, dim):
    return in_order(copy_for_each(array, axis), dim)


def twiddles():
    pulse_ids = jnp.arange(PULSES, dtype=jnp.int32)
    phase_ids = pulse_ids[:, None] * pulse_ids[None, :] % PULSES
    angles = phase_ids.astype(jnp.float32) * (2.0 * jnp.pi / PULSES)
    return jnp.concatenate([jnp.cos(angles), jnp.sin(angles)], axis=0).astype(jnp.bfloat16)


def doppler_spectra(echo_rows, twiddle):
    product = jnp.einsum("kp,rqcp->krqc", twiddle, echo_rows, preferred_element_type=jnp.float32)
    cosine = product[:PULSES]
    sine = product[PULSES:]
    real_part = cosine[:, :, 0] + sine[:, :, 1]
    imag_part = cosine[:, :, 1] - sine[:, :, 0]
    return (
        jnp.stack([real_part, imag_part], axis=2)
        .reshape(PULSES, echo_rows.shape[0], 2 * CH)
        .astype(jnp.bfloat16)
    )


def steering(look_index):
    sines = -1.0 + (2.0 * look_index.astype(jnp.float32) + 1.0) / ANGLES
    channel_ids = jnp.arange(CH).astype(jnp.float32)
    phases = jnp.pi * channel_ids[:, None] * sines[None, :]
    zeros = jnp.zeros((CH, LOOKS), jnp.float32)
    return jnp.stack([zeros, zeros, jnp.cos(phases), jnp.sin(phases), zeros, zeros]).reshape(
        SNAP, LOOKS
    )


def rotate(values):
    return jnp.concatenate([-values[..., CH:], values[..., :CH]], axis=-1)


def upper_blocks(edged, mask_rows):
    bin_count = edged.shape[0] - 2
    rotated = rotate(edged)
    snap = jnp.concatenate([edged[b : b + bin_count] for b in range(3)], axis=-1)
    turned_snap = jnp.concatenate([rotated[b : b + bin_count] for b in range(3)], axis=-1)
    both = jnp.concatenate([snap, turned_snap], axis=1)
    weighting = jnp.concatenate([mask_rows, mask_rows], axis=1)[:, :, None]
    masked = both * weighting
    pieces = []
    for left_pos in range(3):
        pieces.append(
            jnp.einsum(
                "krn,krm->knm",
                masked[:, :, left_pos * 2 * CH : left_pos * 2 * CH + CH],
                both[:, :, left_pos * 2 * CH :],
                preferred_element_type=jnp.float32,
            )
        )
    return jnp.concatenate(pieces, axis=-1)


def full_from_upper(upper):
    width = 2 * CH

    def block(left_pos, right_pos):
        if left_pos > right_pos:
            return jnp.swapaxes(block(right_pos, left_pos), 1, 2)
        start = block_pairs.index((left_pos, right_pos)) * width
        piece = upper[:, :, start : start + width]
        same, cross = piece[..., :CH], piece[..., CH:]
        return jnp.concatenate(
            [jnp.concatenate([same, cross], -1), jnp.concatenate([-cross, same], -1)], 1
        )

    rows = [jnp.concatenate([block(b, c) for c in range(3)], -1) for b in range(3)]
    return jnp.concatenate(rows, 1)


def eliminate(matrix_ref, steer_ref, unit_ref, work_ref):
    rows, cols = work_ref.shape
    matrix = matrix_ref[0]
    steer = steer_ref[...]
    lane_ids = lax.broadcasted_iota(jnp.int32, (1, cols), 1)
    row_ids = lax.broadcasted_iota(jnp.int32, (rows, 1), 0)
    diagonal = row_ids == lane_ids[:, :rows]
    power = jnp.sum(jnp.where(diagonal, matrix, 0.0)) / SNAP + epsilon
    work_ref[:, :rows] = matrix / power + jnp.where(diagonal, loading, 0.0)
    work_ref[:, rows:] = steer

    def step(j, carry):
        current = work_ref[...]
        pivot_row = work_ref[pl.ds(j, 1), :]
        lane_hit = lane_ids == j
        column = jnp.sum(jnp.where(lane_hit, current, 0.0), axis=1, keepdims=True)
        pivot = jnp.sum(jnp.where(lane_hit, pivot_row, 0.0), axis=1, keepdims=True)
        scaled = pivot_row / pivot
        work_ref[...] = jnp.where(row_ids == j, scaled, current - column * scaled)
        return carry

    lax.fori_loop(0, rows, step, 0)
    solved = work_ref[:, rows:]
    gains = jnp.sum(steer * solved, axis=0, keepdims=True)
    unit_ref[0] = (solved / jnp.sqrt(gains)).astype(unit_ref.dtype)


def unit_vectors(matrix, steer):
    count, size, _ = matrix.shape
    return pl.pallas_call(
        eliminate,
        grid=(count,),
        in_specs=[
            pl.BlockSpec((1, size, size), lambda i: (i, 0, 0)),
            pl.BlockSpec((size, LOOKS), lambda i: (0, 0)),
        ],
        out_specs=pl.BlockSpec((1, size, LOOKS), lambda i: (i, 0, 0)),
        out_shape=jax.ShapeDtypeStruct((count, size, LOOKS), jnp.bfloat16),
        scratch_shapes=[pltpu.VMEM((size, size + LOOKS), jnp.float32)],
    )(matrix, steer)


def body(echoes, training, look_index):
    spectra = doppler_spectra(echoes, twiddles())
    turned = lax.all_to_all(spectra, "dop", split_axis=0, concat_axis=1, tiled=True)
    edged = padded(turned, (("dop", 0),), 1)
    bin_count = edged.shape[0] - 2
    upper = upper_blocks(edged, training.astype(jnp.bfloat16))
    my_upper = sum_at_owner(upper, "rng", 0)
    my_unit = unit_vectors(full_from_upper(my_upper), steering(look_index))
    unit = gather_directly(my_unit, "rng", 0)
    shaped = unit.reshape(bin_count, 3, 2, CH, LOOKS)
    rotated = jnp.stack([-shaped[:, :, 1], shaped[:, :, 0]], axis=2).reshape(bin_count, SNAP, LOOKS)
    weights = jnp.concatenate([unit, rotated], axis=2)
    summed = None
    for position in range(3):
        term = jnp.einsum(
            "knj,krn->kjr",
            weights[:, position * 2 * CH : (position + 1) * 2 * CH],
            edged[position : position + bin_count],
            preferred_element_type=jnp.float32,
        )
        summed = term if summed is None else summed + term
    return summed.reshape(bin_count, 2, LOOKS, edged.shape[1])


def solution(mesh):
    in_specs = (P(("rng", "dop"), None, None, None), P("dop", "rng"), P())
    out_specs = P("dop", None, None, "rng")
    return jax.shard_map(body, mesh=mesh, in_specs=in_specs, out_specs=out_specs, check_vma=False)
```

```python
import jax
import jax.numpy as jnp
from jax import lax
from jax.sharding import PartitionSpec as P
from jax.experimental import pallas as pl
from jax.experimental.pallas import tpu as pltpu

CH = 32
PULSES = 128
LOOKS = 64
ANGLES = 256
SNAP = 192


loading = 0.1
epsilon = 1e-06
block_pairs = ((0, 0), (0, 1), (0, 2), (1, 1), (1, 2), (2, 2))


def padded(block, sides, width):
    for axis, dim in sides:
        count = lax.axis_size(axis)
        forward = [(i, i + 1) for i in range(count - 1)]
        forward.append((count - 1, 0))
        backward = [(target, source) for source, target in forward]
        low = lax.ppermute(
            lax.slice_in_dim(block, block.shape[dim] - width, None, axis=dim), axis, forward
        )
        high = lax.ppermute(lax.slice_in_dim(block, 0, width, axis=dim), axis, backward)
        block = jnp.concatenate([low, block, high], axis=dim)
    return block


def split_up(array, dim, count):
    dims = array.shape
    blocks = array.reshape(*dims[:dim], count, dims[dim] // count, *dims[dim + 1 :])
    return jnp.moveaxis(blocks, dim, 0)


def sum_at_owner(array, axis, dim):
    blocks = split_up(array, dim, lax.axis_size(axis))
    arrived = lax.all_to_all(blocks, axis, split_axis=0, concat_axis=0, tiled=True)
    return arrived.sum(axis=0)


def in_order(blocks, dim):
    dims = list(blocks.shape[1:])
    dims[dim] *= blocks.shape[0]
    return jnp.moveaxis(blocks, 0, dim).reshape(dims)


def copy_for_each(array, axis):
    count = lax.axis_size(axis)
    return lax.all_to_all(
        jnp.broadcast_to(array[None], (count, *array.shape)), axis, 0, 0, tiled=True
    )


def gather_directly(array, axis, dim):
    return in_order(copy_for_each(array, axis), dim)


def twiddles():
    pulse_ids = jnp.arange(PULSES, dtype=jnp.int32)
    phase_ids = pulse_ids[:, None] * pulse_ids[None, :] % PULSES
    angles = phase_ids.astype(jnp.float32) * (2.0 * jnp.pi / PULSES)
    return jnp.concatenate([jnp.cos(angles), jnp.sin(angles)], axis=0).astype(jnp.bfloat16)


def doppler_spectra(echo_rows, twiddle):
    product = jnp.einsum("kp,rqcp->krqc", twiddle, echo_rows, preferred_element_type=jnp.float32)
    cosine = product[:PULSES]
    sine = product[PULSES:]
    real_part = cosine[:, :, 0] + sine[:, :, 1]
    imag_part = cosine[:, :, 1] - sine[:, :, 0]
    return (
        jnp.stack([real_part, imag_part], axis=2)
        .reshape(PULSES, echo_rows.shape[0], 2 * CH)
        .astype(jnp.bfloat16)
    )


def steering(look_index):
    sines = -1.0 + (2.0 * look_index.astype(jnp.float32) + 1.0) / ANGLES
    channel_ids = jnp.arange(CH).astype(jnp.float32)
    phases = jnp.pi * channel_ids[:, None] * sines[None, :]
    zeros = jnp.zeros((CH, LOOKS), jnp.float32)
    return jnp.stack([zeros, zeros, jnp.cos(phases), jnp.sin(phases), zeros, zeros]).reshape(
        SNAP, LOOKS
    )


def rotate(values):
    return jnp.concatenate([-values[..., CH:], values[..., :CH]], axis=-1)


def upper_blocks(edged, mask_rows):
    bin_count = edged.shape[0] - 2
    rotated = rotate(edged)
    snap = jnp.concatenate([edged[b : b + bin_count] for b in range(3)], axis=-1)
    turned_snap = jnp.concatenate([rotated[b : b + bin_count] for b in range(3)], axis=-1)
    both = jnp.concatenate([snap, turned_snap], axis=1)
    weighting = jnp.concatenate([mask_rows, mask_rows], axis=1)[:, :, None]
    masked = both * weighting
    pieces = []
    for left_pos in range(3):
        pieces.append(
            jnp.einsum(
                "krn,krm->knm",
                masked[:, :, left_pos * 2 * CH : left_pos * 2 * CH + CH],
                both[:, :, left_pos * 2 * CH :],
                preferred_element_type=jnp.float32,
            )
        )
    return jnp.concatenate(pieces, axis=-1)


def eliminate(real_ref, imag_ref, steer_re_ref, steer_im_ref, unit_ref, wr_ref, wi_ref):
    rows, cols = wr_ref.shape
    gap = cols - LOOKS
    lane_ids = lax.broadcasted_iota(jnp.int32, (1, cols), 1)
    row_ids = lax.broadcasted_iota(jnp.int32, (rows, 1), 0)
    diagonal = row_ids == lax.broadcasted_iota(jnp.int32, (1, rows), 1)
    same = real_ref[0]
    power = 2.0 * jnp.sum(jnp.where(diagonal, same, 0.0)) / SNAP + epsilon
    steer_re = steer_re_ref[...]
    steer_im = steer_im_ref[...]
    wr_ref[...] = jnp.zeros(wr_ref.shape, jnp.float32)
    wi_ref[...] = jnp.zeros(wi_ref.shape, jnp.float32)
    wr_ref[:, :rows] = same / power + jnp.where(diagonal, loading, 0.0)
    wi_ref[:, :rows] = imag_ref[0] / power
    wr_ref[:, gap:] = steer_re
    wi_ref[:, gap:] = steer_im

    def step(j, carry):
        cur_r = wr_ref[...]
        cur_i = wi_ref[...]
        row_r = wr_ref[pl.ds(j, 1), :]
        row_i = wi_ref[pl.ds(j, 1), :]
        hit = lane_ids == j
        col_r = jnp.sum(jnp.where(hit, cur_r, 0.0), axis=1, keepdims=True)
        col_i = jnp.sum(jnp.where(hit, cur_i, 0.0), axis=1, keepdims=True)
        lead_r = jnp.sum(jnp.where(hit, row_r, 0.0), axis=1, keepdims=True)
        lead_i = jnp.sum(jnp.where(hit, row_i, 0.0), axis=1, keepdims=True)
        norm = lead_r * lead_r + lead_i * lead_i
        scaled_r = (row_r * lead_r + row_i * lead_i) / norm
        scaled_i = (row_i * lead_r - row_r * lead_i) / norm
        is_row = row_ids == j
        wr_ref[...] = jnp.where(is_row, scaled_r, cur_r - (col_r * scaled_r - col_i * scaled_i))
        wi_ref[...] = jnp.where(is_row, scaled_i, cur_i - (col_r * scaled_i + col_i * scaled_r))
        return carry

    lax.fori_loop(0, rows, step, 0)
    solved_re = wr_ref[:, gap:]
    solved_im = wi_ref[:, gap:]
    root = jnp.sqrt(jnp.sum(steer_re * solved_re + steer_im * solved_im, axis=0, keepdims=True))
    unit_re = (solved_re / root).astype(unit_ref.dtype)
    unit_im = (solved_im / root).astype(unit_ref.dtype)
    for pos in range(rows // CH):
        unit_ref[0, 2 * pos * CH : (2 * pos + 1) * CH, :] = unit_re[pos * CH : (pos + 1) * CH]
        unit_ref[0, (2 * pos + 1) * CH : (2 * pos + 2) * CH, :] = unit_im[pos * CH : (pos + 1) * CH]


def unit_vectors(same, cross, steer):
    count, size, _ = same.shape
    parts = steer.reshape(size // CH, 2, CH, LOOKS)
    steer_re = parts[:, 0].reshape(size, LOOKS)
    steer_im = parts[:, 1].reshape(size, LOOKS)
    width = ((size + 127) // 128) * 128 + LOOKS
    matrix = pl.BlockSpec((1, size, size), lambda i: (i, 0, 0))
    vector = pl.BlockSpec((size, LOOKS), lambda i: (0, 0))
    return pl.pallas_call(
        eliminate,
        grid=(count,),
        in_specs=[matrix, matrix, vector, vector],
        out_specs=pl.BlockSpec((1, 2 * size, LOOKS), lambda i: (i, 0, 0)),
        out_shape=jax.ShapeDtypeStruct((count, 2 * size, LOOKS), jnp.bfloat16),
        scratch_shapes=[pltpu.VMEM((size, width), jnp.float32)] * 2,
    )(same, cross, steer_re, steer_im)


def hermitian_parts(upper):
    def piece(left_pos, right_pos):
        start = block_pairs.index((left_pos, right_pos)) * 2 * CH
        return upper[:, :, start : start + 2 * CH]

    def real_block(left_pos, right_pos):
        if left_pos > right_pos:
            return jnp.swapaxes(real_block(right_pos, left_pos), 1, 2)
        return piece(left_pos, right_pos)[..., :CH]

    def imag_block(left_pos, right_pos):
        if left_pos > right_pos:
            return -jnp.swapaxes(imag_block(right_pos, left_pos), 1, 2)
        return -piece(left_pos, right_pos)[..., CH:]

    def assemble(block):
        rows = [jnp.concatenate([block(b, c) for c in range(3)], -1) for b in range(3)]
        return jnp.concatenate(rows, 1)

    return assemble(real_block), assemble(imag_block)


def body(echoes, training, look_index):
    spectra = doppler_spectra(echoes, twiddles())
    turned = lax.all_to_all(spectra, "dop", split_axis=0, concat_axis=1, tiled=True)
    edged = padded(turned, (("dop", 0),), 1)
    bin_count = edged.shape[0] - 2
    upper = upper_blocks(edged, training.astype(jnp.bfloat16))
    my_upper = sum_at_owner(upper, "rng", 0)
    my_unit = unit_vectors(*hermitian_parts(my_upper), steering(look_index))
    unit = gather_directly(my_unit, "rng", 0)
    shaped = unit.reshape(bin_count, 3, 2, CH, LOOKS)
    rotated = jnp.stack([-shaped[:, :, 1], shaped[:, :, 0]], axis=2).reshape(bin_count, SNAP, LOOKS)
    weights = jnp.concatenate([unit, rotated], axis=2)
    summed = None
    for position in range(3):
        term = jnp.einsum(
            "knj,krn->kjr",
            weights[:, position * 2 * CH : (position + 1) * 2 * CH],
            edged[position : position + bin_count],
            preferred_element_type=jnp.float32,
        )
        summed = term if summed is None else summed + term
    return summed.reshape(bin_count, 2, LOOKS, edged.shape[1])


def solution(mesh):
    in_specs = (P(("rng", "dop"), None, None, None), P("dop", "rng"), P())
    out_specs = P("dop", None, None, "rng")
    return jax.shard_map(body, mesh=mesh, in_specs=in_specs, out_specs=out_specs, check_vma=False)
```

```python
import jax
import jax.numpy as jnp
from jax import lax
from jax.sharding import PartitionSpec as P
from jax.experimental import pallas as pl
from jax.experimental.pallas import tpu as pltpu

CH = 32
PULSES = 128
LOOKS = 64
ANGLES = 256
SNAP = 192


loading = 0.1
epsilon = 1e-06
block_pairs = ((0, 0), (0, 1), (0, 2), (1, 1), (1, 2), (2, 2))


def padded(block, sides, width):
    for axis, dim in sides:
        count = lax.axis_size(axis)
        forward = [(i, i + 1) for i in range(count - 1)]
        forward.append((count - 1, 0))
        backward = [(target, source) for source, target in forward]
        low = lax.ppermute(
            lax.slice_in_dim(block, block.shape[dim] - width, None, axis=dim), axis, forward
        )
        high = lax.ppermute(lax.slice_in_dim(block, 0, width, axis=dim), axis, backward)
        block = jnp.concatenate([low, block, high], axis=dim)
    return block


def split_up(array, dim, count):
    dims = array.shape
    blocks = array.reshape(*dims[:dim], count, dims[dim] // count, *dims[dim + 1 :])
    return jnp.moveaxis(blocks, dim, 0)


def sum_at_owner(array, axis, dim):
    blocks = split_up(array, dim, lax.axis_size(axis))
    arrived = lax.all_to_all(blocks, axis, split_axis=0, concat_axis=0, tiled=True)
    return arrived.sum(axis=0)


def in_order(blocks, dim):
    dims = list(blocks.shape[1:])
    dims[dim] *= blocks.shape[0]
    return jnp.moveaxis(blocks, 0, dim).reshape(dims)


def copy_for_each(array, axis):
    count = lax.axis_size(axis)
    return lax.all_to_all(
        jnp.broadcast_to(array[None], (count, *array.shape)), axis, 0, 0, tiled=True
    )


def gather_directly(array, axis, dim):
    return in_order(copy_for_each(array, axis), dim)


def twiddles():
    pulse_ids = jnp.arange(PULSES, dtype=jnp.int32)
    phase_ids = pulse_ids[:, None] * pulse_ids[None, :] % PULSES
    angles = phase_ids.astype(jnp.float32) * (2.0 * jnp.pi / PULSES)
    return jnp.concatenate([jnp.cos(angles), jnp.sin(angles)], axis=0).astype(jnp.bfloat16)


def doppler_spectra(echo_rows, twiddle):
    product = jnp.einsum("kp,rqcp->krqc", twiddle, echo_rows, preferred_element_type=jnp.float32)
    cosine = product[:PULSES]
    sine = product[PULSES:]
    real_part = cosine[:, :, 0] + sine[:, :, 1]
    imag_part = cosine[:, :, 1] - sine[:, :, 0]
    return (
        jnp.stack([real_part, imag_part], axis=2)
        .reshape(PULSES, echo_rows.shape[0], 2 * CH)
        .astype(jnp.bfloat16)
    )


def steering(look_index):
    sines = -1.0 + (2.0 * look_index.astype(jnp.float32) + 1.0) / ANGLES
    channel_ids = jnp.arange(CH).astype(jnp.float32)
    phases = jnp.pi * channel_ids[:, None] * sines[None, :]
    zeros = jnp.zeros((CH, LOOKS), jnp.float32)
    return jnp.stack([zeros, zeros, jnp.cos(phases), jnp.sin(phases), zeros, zeros]).reshape(
        SNAP, LOOKS
    )


def rotate(values):
    return jnp.concatenate([-values[..., CH:], values[..., :CH]], axis=-1)


def upper_blocks(edged, mask_rows):
    bin_count = edged.shape[0] - 2
    rotated = rotate(edged)
    snap = jnp.concatenate([edged[b : b + bin_count] for b in range(3)], axis=-1)
    turned_snap = jnp.concatenate([rotated[b : b + bin_count] for b in range(3)], axis=-1)
    both = jnp.concatenate([snap, turned_snap], axis=1)
    weighting = jnp.concatenate([mask_rows, mask_rows], axis=1)[:, :, None]
    masked = both * weighting
    leading = masked.reshape(*masked.shape[:2], 3, 2, CH)[:, :, :, 0].reshape(*masked.shape[:2], 3 * CH)
    return jnp.einsum("krn,krm->knm", leading, both, preferred_element_type=jnp.float32)


def eliminate(real_ref, imag_ref, steer_re_ref, steer_im_ref, unit_ref, wr_ref, wi_ref):
    rows, cols = wr_ref.shape
    gap = cols - LOOKS
    lane_ids = lax.broadcasted_iota(jnp.int32, (1, cols), 1)
    row_ids = lax.broadcasted_iota(jnp.int32, (rows, 1), 0)
    diagonal = row_ids == lax.broadcasted_iota(jnp.int32, (1, rows), 1)
    same = real_ref[0]
    power = 2.0 * jnp.sum(jnp.where(diagonal, same, 0.0)) / SNAP + epsilon
    steer_re = steer_re_ref[...]
    steer_im = steer_im_ref[...]
    wr_ref[...] = jnp.zeros(wr_ref.shape, jnp.float32)
    wi_ref[...] = jnp.zeros(wi_ref.shape, jnp.float32)
    wr_ref[:, :rows] = same / power + jnp.where(diagonal, loading, 0.0)
    wi_ref[:, :rows] = imag_ref[0] / power
    wr_ref[:, gap:] = steer_re
    wi_ref[:, gap:] = steer_im

    def step(j, carry):
        cur_r = wr_ref[...]
        cur_i = wi_ref[...]
        row_r = wr_ref[pl.ds(j, 1), :]
        row_i = wi_ref[pl.ds(j, 1), :]
        hit = lane_ids == j
        col_r = jnp.sum(jnp.where(hit, cur_r, 0.0), axis=1, keepdims=True)
        col_i = jnp.sum(jnp.where(hit, cur_i, 0.0), axis=1, keepdims=True)
        lead_r = jnp.sum(jnp.where(hit, row_r, 0.0), axis=1, keepdims=True)
        lead_i = jnp.sum(jnp.where(hit, row_i, 0.0), axis=1, keepdims=True)
        norm = lead_r * lead_r + lead_i * lead_i
        scaled_r = (row_r * lead_r + row_i * lead_i) / norm
        scaled_i = (row_i * lead_r - row_r * lead_i) / norm
        is_row = row_ids == j
        wr_ref[...] = jnp.where(is_row, scaled_r, cur_r - (col_r * scaled_r - col_i * scaled_i))
        wi_ref[...] = jnp.where(is_row, scaled_i, cur_i - (col_r * scaled_i + col_i * scaled_r))
        return carry

    lax.fori_loop(0, rows, step, 0)
    solved_re = wr_ref[:, gap:]
    solved_im = wi_ref[:, gap:]
    root = jnp.sqrt(jnp.sum(steer_re * solved_re + steer_im * solved_im, axis=0, keepdims=True))
    unit_re = (solved_re / root).astype(unit_ref.dtype)
    unit_im = (solved_im / root).astype(unit_ref.dtype)
    for pos in range(rows // CH):
        unit_ref[0, 2 * pos * CH : (2 * pos + 1) * CH, :] = unit_re[pos * CH : (pos + 1) * CH]
        unit_ref[0, (2 * pos + 1) * CH : (2 * pos + 2) * CH, :] = unit_im[pos * CH : (pos + 1) * CH]


def unit_vectors(same, cross, steer):
    count, size, _ = same.shape
    parts = steer.reshape(size // CH, 2, CH, LOOKS)
    steer_re = parts[:, 0].reshape(size, LOOKS)
    steer_im = parts[:, 1].reshape(size, LOOKS)
    width = ((size + 127) // 128) * 128 + LOOKS
    matrix = pl.BlockSpec((1, size, size), lambda i: (i, 0, 0))
    vector = pl.BlockSpec((size, LOOKS), lambda i: (0, 0))
    return pl.pallas_call(
        eliminate,
        grid=(count,),
        in_specs=[matrix, matrix, vector, vector],
        out_specs=pl.BlockSpec((1, 2 * size, LOOKS), lambda i: (i, 0, 0)),
        out_shape=jax.ShapeDtypeStruct((count, 2 * size, LOOKS), jnp.bfloat16),
        scratch_shapes=[pltpu.VMEM((size, width), jnp.float32)] * 2,
    )(same, cross, steer_re, steer_im)


def hermitian_parts(rows):
    split = rows.reshape(rows.shape[0], rows.shape[1], 3, 2, CH)
    size = rows.shape[1]
    return split[:, :, :, 0].reshape(-1, size, size), -split[:, :, :, 1].reshape(-1, size, size)


def body(echoes, training, look_index):
    spectra = doppler_spectra(echoes, twiddles())
    turned = lax.all_to_all(spectra, "dop", split_axis=0, concat_axis=1, tiled=True)
    edged = padded(turned, (("dop", 0),), 1)
    bin_count = edged.shape[0] - 2
    upper = upper_blocks(edged, training.astype(jnp.bfloat16))
    my_upper = sum_at_owner(upper, "rng", 0)
    my_unit = unit_vectors(*hermitian_parts(my_upper), steering(look_index))
    unit = gather_directly(my_unit, "rng", 0)
    shaped = unit.reshape(bin_count, 3, 2, CH, LOOKS)
    rotated = jnp.stack([-shaped[:, :, 1], shaped[:, :, 0]], axis=2).reshape(bin_count, SNAP, LOOKS)
    weights = jnp.concatenate([unit, rotated], axis=2)
    summed = None
    for position in range(3):
        term = jnp.einsum(
            "knj,krn->kjr",
            weights[:, position * 2 * CH : (position + 1) * 2 * CH],
            edged[position : position + bin_count],
            preferred_element_type=jnp.float32,
        )
        summed = term if summed is None else summed + term
    return summed.reshape(bin_count, 2, LOOKS, edged.shape[1])


def solution(mesh):
    in_specs = (P(("rng", "dop"), None, None, None), P("dop", "rng"), P())
    out_specs = P("dop", None, None, "rng")
    return jax.shard_map(body, mesh=mesh, in_specs=in_specs, out_specs=out_specs, check_vma=False)
```

```python
import jax
import jax.numpy as jnp
from jax import lax
from jax.sharding import PartitionSpec as P
from jax.experimental import pallas as pl
from jax.experimental.pallas import tpu as pltpu

CH = 32
PULSES = 128
LOOKS = 64
ANGLES = 256
SNAP = 192


loading = 0.1
epsilon = 1e-06
block_pairs = ((0, 0), (0, 1), (0, 2), (1, 1), (1, 2), (2, 2))


def padded(block, sides, width):
    for axis, dim in sides:
        count = lax.axis_size(axis)
        forward = [(i, i + 1) for i in range(count - 1)]
        forward.append((count - 1, 0))
        backward = [(target, source) for source, target in forward]
        low = lax.ppermute(
            lax.slice_in_dim(block, block.shape[dim] - width, None, axis=dim), axis, forward
        )
        high = lax.ppermute(lax.slice_in_dim(block, 0, width, axis=dim), axis, backward)
        block = jnp.concatenate([low, block, high], axis=dim)
    return block


def split_up(array, dim, count):
    dims = array.shape
    blocks = array.reshape(*dims[:dim], count, dims[dim] // count, *dims[dim + 1 :])
    return jnp.moveaxis(blocks, dim, 0)


def sum_at_owner(array, axis, dim):
    blocks = split_up(array, dim, lax.axis_size(axis))
    arrived = lax.all_to_all(blocks, axis, split_axis=0, concat_axis=0, tiled=True)
    return arrived.sum(axis=0)


def in_order(blocks, dim):
    dims = list(blocks.shape[1:])
    dims[dim] *= blocks.shape[0]
    return jnp.moveaxis(blocks, 0, dim).reshape(dims)


def copy_for_each(array, axis):
    count = lax.axis_size(axis)
    return lax.all_to_all(
        jnp.broadcast_to(array[None], (count, *array.shape)), axis, 0, 0, tiled=True
    )


def gather_directly(array, axis, dim):
    return in_order(copy_for_each(array, axis), dim)


def twiddles():
    pulse_ids = jnp.arange(PULSES, dtype=jnp.int32)
    phase_ids = pulse_ids[:, None] * pulse_ids[None, :] % PULSES
    angles = phase_ids.astype(jnp.float32) * (2.0 * jnp.pi / PULSES)
    return jnp.concatenate([jnp.cos(angles), jnp.sin(angles)], axis=0).astype(jnp.bfloat16)


def doppler_spectra(echo_rows, twiddle):
    product = jnp.einsum("kp,rqcp->krqc", twiddle, echo_rows, preferred_element_type=jnp.float32)
    cosine = product[:PULSES]
    sine = product[PULSES:]
    real_part = cosine[:, :, 0] + sine[:, :, 1]
    imag_part = cosine[:, :, 1] - sine[:, :, 0]
    return (
        jnp.stack([real_part, imag_part], axis=2)
        .reshape(PULSES, echo_rows.shape[0], 2 * CH)
        .astype(jnp.bfloat16)
    )


def steering(look_index):
    sines = -1.0 + (2.0 * look_index.astype(jnp.float32) + 1.0) / ANGLES
    channel_ids = jnp.arange(CH).astype(jnp.float32)
    phases = jnp.pi * channel_ids[:, None] * sines[None, :]
    zeros = jnp.zeros((CH, LOOKS), jnp.float32)
    return jnp.stack([zeros, zeros, jnp.cos(phases), jnp.sin(phases), zeros, zeros]).reshape(
        SNAP, LOOKS
    )


def rotate(values):
    return jnp.concatenate([-values[..., CH:], values[..., :CH]], axis=-1)


def upper_blocks(edged, mask_rows):
    bin_count = edged.shape[0] - 2
    rotated = rotate(edged)
    snap = jnp.concatenate([edged[b : b + bin_count] for b in range(3)], axis=-1)
    turned_snap = jnp.concatenate([rotated[b : b + bin_count] for b in range(3)], axis=-1)
    both = jnp.concatenate([snap, turned_snap], axis=1)
    weighting = jnp.concatenate([mask_rows, mask_rows], axis=1)[:, :, None]
    masked = both * weighting
    below = lax.broadcasted_iota(jnp.int32, (CH, CH), 0) > lax.broadcasted_iota(jnp.int32, (CH, CH), 1)
    pieces = []
    for left_pos in range(3):
        start = left_pos * 2 * CH
        piece = jnp.einsum(
            "krn,krm->knm",
            masked[:, :, start : start + CH],
            both[:, :, start:],
            preferred_element_type=jnp.float32,
        )
        folded = jnp.where(below, piece[..., CH : 2 * CH], piece[..., :CH])
        pieces.extend([folded, piece[..., 2 * CH :]])
    return jnp.concatenate(pieces, axis=-1)


def eliminate(real_ref, imag_ref, steer_re_ref, steer_im_ref, unit_ref, wr_ref, wi_ref):
    rows, cols = wr_ref.shape
    gap = cols - LOOKS
    lane_ids = lax.broadcasted_iota(jnp.int32, (1, cols), 1)
    row_ids = lax.broadcasted_iota(jnp.int32, (rows, 1), 0)
    diagonal = row_ids == lax.broadcasted_iota(jnp.int32, (1, rows), 1)
    same = real_ref[0]
    power = 2.0 * jnp.sum(jnp.where(diagonal, same, 0.0)) / SNAP + epsilon
    steer_re = steer_re_ref[...]
    steer_im = steer_im_ref[...]
    wr_ref[...] = jnp.zeros(wr_ref.shape, jnp.float32)
    wi_ref[...] = jnp.zeros(wi_ref.shape, jnp.float32)
    wr_ref[:, :rows] = same / power + jnp.where(diagonal, loading, 0.0)
    wi_ref[:, :rows] = imag_ref[0] / power
    wr_ref[:, gap:] = steer_re
    wi_ref[:, gap:] = steer_im

    def step(j, carry):
        cur_r = wr_ref[...]
        cur_i = wi_ref[...]
        row_r = wr_ref[pl.ds(j, 1), :]
        row_i = wi_ref[pl.ds(j, 1), :]
        hit = lane_ids == j
        col_r = jnp.sum(jnp.where(hit, cur_r, 0.0), axis=1, keepdims=True)
        col_i = jnp.sum(jnp.where(hit, cur_i, 0.0), axis=1, keepdims=True)
        lead_r = jnp.sum(jnp.where(hit, row_r, 0.0), axis=1, keepdims=True)
        lead_i = jnp.sum(jnp.where(hit, row_i, 0.0), axis=1, keepdims=True)
        norm = lead_r * lead_r + lead_i * lead_i
        scaled_r = (row_r * lead_r + row_i * lead_i) / norm
        scaled_i = (row_i * lead_r - row_r * lead_i) / norm
        is_row = row_ids == j
        wr_ref[...] = jnp.where(is_row, scaled_r, cur_r - (col_r * scaled_r - col_i * scaled_i))
        wi_ref[...] = jnp.where(is_row, scaled_i, cur_i - (col_r * scaled_i + col_i * scaled_r))
        return carry

    lax.fori_loop(0, rows, step, 0)
    solved_re = wr_ref[:, gap:]
    solved_im = wi_ref[:, gap:]
    root = jnp.sqrt(jnp.sum(steer_re * solved_re + steer_im * solved_im, axis=0, keepdims=True))
    unit_re = (solved_re / root).astype(unit_ref.dtype)
    unit_im = (solved_im / root).astype(unit_ref.dtype)
    for pos in range(rows // CH):
        unit_ref[0, 2 * pos * CH : (2 * pos + 1) * CH, :] = unit_re[pos * CH : (pos + 1) * CH]
        unit_ref[0, (2 * pos + 1) * CH : (2 * pos + 2) * CH, :] = unit_im[pos * CH : (pos + 1) * CH]


def unit_vectors(same, cross, steer):
    count, size, _ = same.shape
    parts = steer.reshape(size // CH, 2, CH, LOOKS)
    steer_re = parts[:, 0].reshape(size, LOOKS)
    steer_im = parts[:, 1].reshape(size, LOOKS)
    width = ((size + 127) // 128) * 128 + LOOKS
    matrix = pl.BlockSpec((1, size, size), lambda i: (i, 0, 0))
    vector = pl.BlockSpec((size, LOOKS), lambda i: (0, 0))
    return pl.pallas_call(
        eliminate,
        grid=(count,),
        in_specs=[matrix, matrix, vector, vector],
        out_specs=pl.BlockSpec((1, 2 * size, LOOKS), lambda i: (i, 0, 0)),
        out_shape=jax.ShapeDtypeStruct((count, 2 * size, LOOKS), jnp.bfloat16),
        scratch_shapes=[pltpu.VMEM((size, width), jnp.float32)] * 2,
    )(same, cross, steer_re, steer_im)


def hermitian_parts(upper):
    below = lax.broadcasted_iota(jnp.int32, (CH, CH), 0) > lax.broadcasted_iota(jnp.int32, (CH, CH), 1)
    starts = {}
    offset = 0
    for left_pos in range(3):
        starts[left_pos] = offset
        offset += CH + (2 - left_pos) * 2 * CH

    def real_block(left_pos, right_pos):
        if left_pos > right_pos:
            return jnp.swapaxes(real_block(right_pos, left_pos), 1, 2)
        start = starts[left_pos]
        if left_pos == right_pos:
            folded = upper[:, :, start : start + CH]
            return jnp.where(below, jnp.swapaxes(folded, 1, 2), folded)
        start += CH + (right_pos - left_pos - 1) * 2 * CH
        return upper[:, :, start : start + CH]

    def imag_block(left_pos, right_pos):
        if left_pos > right_pos:
            return -jnp.swapaxes(imag_block(right_pos, left_pos), 1, 2)
        start = starts[left_pos]
        if left_pos == right_pos:
            folded = upper[:, :, start : start + CH]
            above = jnp.swapaxes(below, 0, 1)
            return jnp.where(below, -folded, jnp.where(above, jnp.swapaxes(folded, 1, 2), 0.0))
        start += CH + (right_pos - left_pos - 1) * 2 * CH
        return -upper[:, :, start + CH : start + 2 * CH]

    def assemble(block):
        rows = [jnp.concatenate([block(b, c) for c in range(3)], -1) for b in range(3)]
        return jnp.concatenate(rows, 1)

    return assemble(real_block), assemble(imag_block)


def body(echoes, training, look_index):
    spectra = doppler_spectra(echoes, twiddles())
    turned = lax.all_to_all(spectra, "dop", split_axis=0, concat_axis=1, tiled=True)
    edged = padded(turned, (("dop", 0),), 1)
    bin_count = edged.shape[0] - 2
    upper = upper_blocks(edged, training.astype(jnp.bfloat16))
    my_upper = sum_at_owner(upper, "rng", 0)
    my_unit = unit_vectors(*hermitian_parts(my_upper), steering(look_index))
    unit = gather_directly(my_unit, "rng", 0)
    shaped = unit.reshape(bin_count, 3, 2, CH, LOOKS)
    rotated = jnp.stack([-shaped[:, :, 1], shaped[:, :, 0]], axis=2).reshape(bin_count, SNAP, LOOKS)
    weights = jnp.concatenate([unit, rotated], axis=2)
    summed = None
    for position in range(3):
        term = jnp.einsum(
            "knj,krn->kjr",
            weights[:, position * 2 * CH : (position + 1) * 2 * CH],
            edged[position : position + bin_count],
            preferred_element_type=jnp.float32,
        )
        summed = term if summed is None else summed + term
    return summed.reshape(bin_count, 2, LOOKS, edged.shape[1])


def solution(mesh):
    in_specs = (P(("rng", "dop"), None, None, None), P("dop", "rng"), P())
    out_specs = P("dop", None, None, "rng")
    return jax.shard_map(body, mesh=mesh, in_specs=in_specs, out_specs=out_specs, check_vma=False)
```

```python
import jax
import jax.numpy as jnp
from jax import lax
from jax.sharding import PartitionSpec as P
from jax.experimental import pallas as pl
from jax.experimental.pallas import tpu as pltpu

CH = 32
PULSES = 128
LOOKS = 64
ANGLES = 256
SNAP = 192


loading = 0.1
epsilon = 1e-06
block_pairs = ((0, 0), (0, 1), (0, 2), (1, 1), (1, 2), (2, 2))


def padded(block, sides, width):
    for axis, dim in sides:
        count = lax.axis_size(axis)
        forward = [(i, i + 1) for i in range(count - 1)]
        forward.append((count - 1, 0))
        backward = [(target, source) for source, target in forward]
        low = lax.ppermute(
            lax.slice_in_dim(block, block.shape[dim] - width, None, axis=dim), axis, forward
        )
        high = lax.ppermute(lax.slice_in_dim(block, 0, width, axis=dim), axis, backward)
        block = jnp.concatenate([low, block, high], axis=dim)
    return block


def split_up(array, dim, count):
    dims = array.shape
    blocks = array.reshape(*dims[:dim], count, dims[dim] // count, *dims[dim + 1 :])
    return jnp.moveaxis(blocks, dim, 0)


def sum_at_owner(array, axis, dim):
    blocks = split_up(array, dim, lax.axis_size(axis))
    arrived = lax.all_to_all(blocks, axis, split_axis=0, concat_axis=0, tiled=True)
    return arrived.sum(axis=0)


def in_order(blocks, dim):
    dims = list(blocks.shape[1:])
    dims[dim] *= blocks.shape[0]
    return jnp.moveaxis(blocks, 0, dim).reshape(dims)


def copy_for_each(array, axis):
    count = lax.axis_size(axis)
    return lax.all_to_all(
        jnp.broadcast_to(array[None], (count, *array.shape)), axis, 0, 0, tiled=True
    )


def gather_directly(array, axis, dim):
    return in_order(copy_for_each(array, axis), dim)


def twiddles():
    pulse_ids = jnp.arange(PULSES, dtype=jnp.int32)
    phase_ids = pulse_ids[:, None] * pulse_ids[None, :] % PULSES
    angles = phase_ids.astype(jnp.float32) * (2.0 * jnp.pi / PULSES)
    return jnp.concatenate([jnp.cos(angles), jnp.sin(angles)], axis=0).astype(jnp.bfloat16)


def transform(twiddle_ref, echo_ref, out_ref):
    rows = echo_ref.shape[0]
    echoes = echo_ref[...]
    swapped = jnp.stack([echoes[:, 1], -echoes[:, 0]], axis=1)
    stacked = jnp.concatenate(
        [echoes.reshape(rows * 2 * CH, PULSES), swapped.reshape(rows * 2 * CH, PULSES)], axis=1
    )
    out_ref[...] = lax.dot_general(
        twiddle_ref[...], stacked, (((1,), (1,)), ((), ())), preferred_element_type=jnp.float32
    ).astype(out_ref.dtype)

def doppler_spectra(echo_rows, twiddle):
    rows = echo_rows.shape[0]
    paired = jnp.concatenate([twiddle[:PULSES], twiddle[PULSES:]], axis=1)
    return pl.pallas_call(
        transform,
        out_shape=jax.ShapeDtypeStruct((PULSES, rows * 2 * CH), jnp.bfloat16),
    )(paired, echo_rows)

def steering(look_index):
    sines = -1.0 + (2.0 * look_index.astype(jnp.float32) + 1.0) / ANGLES
    channel_ids = jnp.arange(CH).astype(jnp.float32)
    phases = jnp.pi * channel_ids[:, None] * sines[None, :]
    zeros = jnp.zeros((CH, LOOKS), jnp.float32)
    return jnp.stack([zeros, zeros, jnp.cos(phases), jnp.sin(phases), zeros, zeros]).reshape(
        SNAP, LOOKS
    )


def rotate(values):
    return jnp.concatenate([-values[..., CH:], values[..., :CH]], axis=-1)


def upper_blocks(edged, mask_rows):
    bin_count = edged.shape[0] - 2
    rotated = rotate(edged)
    snap = jnp.concatenate([edged[b : b + bin_count] for b in range(3)], axis=-1)
    turned_snap = jnp.concatenate([rotated[b : b + bin_count] for b in range(3)], axis=-1)
    both = jnp.concatenate([snap, turned_snap], axis=1)
    weighting = jnp.concatenate([mask_rows, mask_rows], axis=1)[:, :, None]
    masked = both * weighting
    pieces = []
    for left_pos in range(3):
        pieces.append(
            jnp.einsum(
                "krn,krm->knm",
                masked[:, :, left_pos * 2 * CH : left_pos * 2 * CH + CH],
                both[:, :, left_pos * 2 * CH :],
                preferred_element_type=jnp.float32,
            )
        )
    return jnp.concatenate(pieces, axis=-1)


def eliminate(real_ref, imag_ref, steer_re_ref, steer_im_ref, unit_ref, wr_ref, wi_ref):
    rows, cols = wr_ref.shape
    gap = cols - LOOKS
    lane_ids = lax.broadcasted_iota(jnp.int32, (1, cols), 1)
    row_ids = lax.broadcasted_iota(jnp.int32, (rows, 1), 0)
    diagonal = row_ids == lax.broadcasted_iota(jnp.int32, (1, rows), 1)
    same = real_ref[0]
    power = 2.0 * jnp.sum(jnp.where(diagonal, same, 0.0)) / SNAP + epsilon
    steer_re = steer_re_ref[...]
    steer_im = steer_im_ref[...]
    wr_ref[...] = jnp.zeros(wr_ref.shape, jnp.float32)
    wi_ref[...] = jnp.zeros(wi_ref.shape, jnp.float32)
    wr_ref[:, :rows] = same / power + jnp.where(diagonal, loading, 0.0)
    wi_ref[:, :rows] = imag_ref[0] / power
    wr_ref[:, gap:] = steer_re
    wi_ref[:, gap:] = steer_im

    def step(j, carry):
        cur_r = wr_ref[...]
        cur_i = wi_ref[...]
        row_r = wr_ref[pl.ds(j, 1), :]
        row_i = wi_ref[pl.ds(j, 1), :]
        hit = lane_ids == j
        col_r = jnp.sum(jnp.where(hit, cur_r, 0.0), axis=1, keepdims=True)
        col_i = jnp.sum(jnp.where(hit, cur_i, 0.0), axis=1, keepdims=True)
        lead_r = jnp.sum(jnp.where(hit, row_r, 0.0), axis=1, keepdims=True)
        lead_i = jnp.sum(jnp.where(hit, row_i, 0.0), axis=1, keepdims=True)
        norm = lead_r * lead_r + lead_i * lead_i
        scaled_r = (row_r * lead_r + row_i * lead_i) / norm
        scaled_i = (row_i * lead_r - row_r * lead_i) / norm
        is_row = row_ids == j
        wr_ref[...] = jnp.where(is_row, scaled_r, cur_r - (col_r * scaled_r - col_i * scaled_i))
        wi_ref[...] = jnp.where(is_row, scaled_i, cur_i - (col_r * scaled_i + col_i * scaled_r))
        return carry

    lax.fori_loop(0, rows, step, 0)
    solved_re = wr_ref[:, gap:]
    solved_im = wi_ref[:, gap:]
    root = jnp.sqrt(jnp.sum(steer_re * solved_re + steer_im * solved_im, axis=0, keepdims=True))
    unit_re = (solved_re / root).astype(unit_ref.dtype)
    unit_im = (solved_im / root).astype(unit_ref.dtype)
    for pos in range(rows // CH):
        unit_ref[0, 2 * pos * CH : (2 * pos + 1) * CH, :] = unit_re[pos * CH : (pos + 1) * CH]
        unit_ref[0, (2 * pos + 1) * CH : (2 * pos + 2) * CH, :] = unit_im[pos * CH : (pos + 1) * CH]


def unit_vectors(same, cross, steer):
    count, size, _ = same.shape
    parts = steer.reshape(size // CH, 2, CH, LOOKS)
    steer_re = parts[:, 0].reshape(size, LOOKS)
    steer_im = parts[:, 1].reshape(size, LOOKS)
    width = ((size + 127) // 128) * 128 + LOOKS
    matrix = pl.BlockSpec((1, size, size), lambda i: (i, 0, 0))
    vector = pl.BlockSpec((size, LOOKS), lambda i: (0, 0))
    return pl.pallas_call(
        eliminate,
        grid=(count,),
        in_specs=[matrix, matrix, vector, vector],
        out_specs=pl.BlockSpec((1, 2 * size, LOOKS), lambda i: (i, 0, 0)),
        out_shape=jax.ShapeDtypeStruct((count, 2 * size, LOOKS), jnp.bfloat16),
        scratch_shapes=[pltpu.VMEM((size, width), jnp.float32)] * 2,
    )(same, cross, steer_re, steer_im)


def hermitian_parts(upper):
    def piece(left_pos, right_pos):
        start = block_pairs.index((left_pos, right_pos)) * 2 * CH
        return upper[:, :, start : start + 2 * CH]

    def real_block(left_pos, right_pos):
        if left_pos > right_pos:
            return jnp.swapaxes(real_block(right_pos, left_pos), 1, 2)
        return piece(left_pos, right_pos)[..., :CH]

    def imag_block(left_pos, right_pos):
        if left_pos > right_pos:
            return -jnp.swapaxes(imag_block(right_pos, left_pos), 1, 2)
        return -piece(left_pos, right_pos)[..., CH:]

    def assemble(block):
        rows = [jnp.concatenate([block(b, c) for c in range(3)], -1) for b in range(3)]
        return jnp.concatenate(rows, 1)

    return assemble(real_block), assemble(imag_block)


def body(echoes, training, look_index):
    spectra = doppler_spectra(echoes, twiddles())
    turned = lax.all_to_all(spectra, "dop", split_axis=0, concat_axis=1, tiled=True)
    turned = turned.reshape(turned.shape[0], -1, 2 * CH)
    edged = padded(turned, (("dop", 0),), 1)
    bin_count = edged.shape[0] - 2
    upper = upper_blocks(edged, training.astype(jnp.bfloat16))
    my_upper = sum_at_owner(upper, "rng", 0)
    my_unit = unit_vectors(*hermitian_parts(my_upper), steering(look_index))
    unit = gather_directly(my_unit, "rng", 0)
    shaped = unit.reshape(bin_count, 3, 2, CH, LOOKS)
    rotated = jnp.stack([-shaped[:, :, 1], shaped[:, :, 0]], axis=2).reshape(bin_count, SNAP, LOOKS)
    weights = jnp.concatenate([unit, rotated], axis=2)
    summed = None
    for position in range(3):
        term = jnp.einsum(
            "knj,krn->kjr",
            weights[:, position * 2 * CH : (position + 1) * 2 * CH],
            edged[position : position + bin_count],
            preferred_element_type=jnp.float32,
        )
        summed = term if summed is None else summed + term
    return summed.reshape(bin_count, 2, LOOKS, edged.shape[1])


def solution(mesh):
    in_specs = (P(("rng", "dop"), None, None, None), P("dop", "rng"), P())
    out_specs = P("dop", None, None, "rng")
    return jax.shard_map(body, mesh=mesh, in_specs=in_specs, out_specs=out_specs, check_vma=False)
```

```python
import jax
import jax.numpy as jnp
from jax import lax
from jax.sharding import PartitionSpec as P
from jax.experimental import pallas as pl
from jax.experimental.pallas import tpu as pltpu

CH = 32
PULSES = 128
LOOKS = 64
ANGLES = 256
SNAP = 192


loading = 0.1
epsilon = 1e-06
block_pairs = ((0, 0), (0, 1), (0, 2), (1, 1), (1, 2), (2, 2))


def padded(block, sides, width):
    for axis, dim in sides:
        count = lax.axis_size(axis)
        forward = [(i, i + 1) for i in range(count - 1)]
        forward.append((count - 1, 0))
        backward = [(target, source) for source, target in forward]
        low = lax.ppermute(
            lax.slice_in_dim(block, block.shape[dim] - width, None, axis=dim), axis, forward
        )
        high = lax.ppermute(lax.slice_in_dim(block, 0, width, axis=dim), axis, backward)
        block = jnp.concatenate([low, block, high], axis=dim)
    return block


def split_up(array, dim, count):
    dims = array.shape
    blocks = array.reshape(*dims[:dim], count, dims[dim] // count, *dims[dim + 1 :])
    return jnp.moveaxis(blocks, dim, 0)


def sum_at_owner(array, axis, dim):
    blocks = split_up(array, dim, lax.axis_size(axis))
    arrived = lax.all_to_all(blocks, axis, split_axis=0, concat_axis=0, tiled=True)
    return arrived.sum(axis=0)


def in_order(blocks, dim):
    dims = list(blocks.shape[1:])
    dims[dim] *= blocks.shape[0]
    return jnp.moveaxis(blocks, 0, dim).reshape(dims)


def copy_for_each(array, axis):
    count = lax.axis_size(axis)
    return lax.all_to_all(
        jnp.broadcast_to(array[None], (count, *array.shape)), axis, 0, 0, tiled=True
    )


def gather_directly(array, axis, dim):
    return in_order(copy_for_each(array, axis), dim)


def twiddles():
    pulse_ids = jnp.arange(PULSES, dtype=jnp.int32)
    phase_ids = pulse_ids[:, None] * pulse_ids[None, :] % PULSES
    angles = phase_ids.astype(jnp.float32) * (2.0 * jnp.pi / PULSES)
    return jnp.concatenate([jnp.cos(angles), jnp.sin(angles)], axis=0).astype(jnp.bfloat16)


def transform(twiddle_ref, echo_ref, out_ref):
    rows = echo_ref.shape[0]
    echoes = echo_ref[...]
    swapped = jnp.stack([echoes[:, 1], -echoes[:, 0]], axis=1)
    stacked = jnp.concatenate(
        [echoes.reshape(rows * 2 * CH, PULSES), swapped.reshape(rows * 2 * CH, PULSES)], axis=1
    )
    out_ref[...] = lax.dot_general(
        twiddle_ref[...], stacked, (((1,), (1,)), ((), ())), preferred_element_type=jnp.float32
    ).astype(out_ref.dtype)

def doppler_spectra(echo_rows, twiddle):
    rows = echo_rows.shape[0]
    paired = jnp.concatenate([twiddle[:PULSES], twiddle[PULSES:]], axis=1)
    return pl.pallas_call(
        transform,
        out_shape=jax.ShapeDtypeStruct((PULSES, rows * 2 * CH), jnp.bfloat16),
    )(paired, echo_rows)

def steering(look_index):
    sines = -1.0 + (2.0 * look_index.astype(jnp.float32) + 1.0) / ANGLES
    channel_ids = jnp.arange(CH).astype(jnp.float32)
    phases = jnp.pi * channel_ids[:, None] * sines[None, :]
    zeros = jnp.zeros((CH, LOOKS), jnp.float32)
    return jnp.stack([zeros, zeros, jnp.cos(phases), jnp.sin(phases), zeros, zeros]).reshape(
        SNAP, LOOKS
    )


def rotate(values):
    return jnp.concatenate([-values[..., CH:], values[..., :CH]], axis=-1)


def upper_blocks(edged, mask_rows):
    bin_count = edged.shape[0] - 2
    rotated = rotate(edged)
    snap = jnp.concatenate([edged[b : b + bin_count] for b in range(3)], axis=-1)
    turned_snap = jnp.concatenate([rotated[b : b + bin_count] for b in range(3)], axis=-1)
    both = jnp.concatenate([snap, turned_snap], axis=1)
    weighting = jnp.concatenate([mask_rows, mask_rows], axis=1)[:, :, None]
    masked = both * weighting
    pieces = []
    for left_pos in range(3):
        pieces.append(
            jnp.einsum(
                "krn,krm->knm",
                masked[:, :, left_pos * 2 * CH : left_pos * 2 * CH + CH],
                both[:, :, left_pos * 2 * CH :],
                preferred_element_type=jnp.float32,
            )
        )
    return jnp.concatenate(pieces, axis=-1)


def eliminate(real_ref, imag_ref, steer_re_ref, steer_im_ref, unit_ref, wr_ref, wi_ref):
    rows, cols = wr_ref.shape
    gap = cols - LOOKS
    lane_ids = lax.broadcasted_iota(jnp.int32, (1, cols), 1)
    row_ids = lax.broadcasted_iota(jnp.int32, (rows, 1), 0)
    diagonal = row_ids == lax.broadcasted_iota(jnp.int32, (1, rows), 1)
    same = real_ref[0]
    power = 2.0 * jnp.sum(jnp.where(diagonal, same, 0.0)) / SNAP + epsilon
    steer_re = steer_re_ref[...]
    steer_im = steer_im_ref[...]
    wr_ref[...] = jnp.zeros(wr_ref.shape, jnp.float32)
    wi_ref[...] = jnp.zeros(wi_ref.shape, jnp.float32)
    wr_ref[:, :rows] = same / power + jnp.where(diagonal, loading, 0.0)
    wi_ref[:, :rows] = imag_ref[0] / power
    wr_ref[:, gap:] = steer_re
    wi_ref[:, gap:] = steer_im

    def pick(values, hit):
        return jnp.sum(jnp.where(hit, values, 0.0), axis=1, keepdims=True)

    def times(a_r, a_i, b_r, b_i):
        return a_r * b_r - a_i * b_i, a_r * b_i + a_i * b_r

    def step(half, carry):
        j = 2 * half
        cur_r = wr_ref[...]
        cur_i = wi_ref[...]
        top_r = wr_ref[pl.ds(j, 1), :]
        top_i = wi_ref[pl.ds(j, 1), :]
        low_r = wr_ref[pl.ds(j + 1, 1), :]
        low_i = wi_ref[pl.ds(j + 1, 1), :]
        first = lane_ids == j
        second = lane_ids == j + 1
        a_r, a_i = pick(top_r, first), pick(top_i, first)
        b_r, b_i = pick(top_r, second), pick(top_i, second)
        c_r, c_i = pick(low_r, first), pick(low_i, first)
        d_r, d_i = pick(low_r, second), pick(low_i, second)
        ad_r, ad_i = times(a_r, a_i, d_r, d_i)
        bc_r, bc_i = times(b_r, b_i, c_r, c_i)
        det_r, det_i = ad_r - bc_r, ad_i - bc_i
        scale = 1.0 / (det_r * det_r + det_i * det_i)
        inv_r, inv_i = det_r * scale, -det_i * scale
        p_r, p_i = times(d_r, d_i, top_r, top_i)
        q_r, q_i = times(b_r, b_i, low_r, low_i)
        one_r, one_i = times(inv_r, inv_i, p_r - q_r, p_i - q_i)
        s_r, s_i = times(a_r, a_i, low_r, low_i)
        t_r, t_i = times(c_r, c_i, top_r, top_i)
        two_r, two_i = times(inv_r, inv_i, s_r - t_r, s_i - t_i)
        u_r, u_i = pick(cur_r, first), pick(cur_i, first)
        v_r, v_i = pick(cur_r, second), pick(cur_i, second)
        x_r, x_i = times(u_r, u_i, one_r, one_i)
        y_r, y_i = times(v_r, v_i, two_r, two_i)
        wr_ref[...] = cur_r - (x_r + y_r)
        wi_ref[...] = cur_i - (x_i + y_i)
        wr_ref[pl.ds(j, 1), :] = one_r
        wi_ref[pl.ds(j, 1), :] = one_i
        wr_ref[pl.ds(j + 1, 1), :] = two_r
        wi_ref[pl.ds(j + 1, 1), :] = two_i
        return carry

    lax.fori_loop(0, rows // 2, step, 0)
    solved_re = wr_ref[:, gap:]
    solved_im = wi_ref[:, gap:]
    root = jnp.sqrt(jnp.sum(steer_re * solved_re + steer_im * solved_im, axis=0, keepdims=True))
    unit_re = (solved_re / root).astype(unit_ref.dtype)
    unit_im = (solved_im / root).astype(unit_ref.dtype)
    for pos in range(rows // CH):
        unit_ref[0, 2 * pos * CH : (2 * pos + 1) * CH, :] = unit_re[pos * CH : (pos + 1) * CH]
        unit_ref[0, (2 * pos + 1) * CH : (2 * pos + 2) * CH, :] = unit_im[pos * CH : (pos + 1) * CH]

def unit_vectors(same, cross, steer):
    count, size, _ = same.shape
    parts = steer.reshape(size // CH, 2, CH, LOOKS)
    steer_re = parts[:, 0].reshape(size, LOOKS)
    steer_im = parts[:, 1].reshape(size, LOOKS)
    width = ((size + 127) // 128) * 128 + LOOKS
    matrix = pl.BlockSpec((1, size, size), lambda i: (i, 0, 0))
    vector = pl.BlockSpec((size, LOOKS), lambda i: (0, 0))
    return pl.pallas_call(
        eliminate,
        grid=(count,),
        in_specs=[matrix, matrix, vector, vector],
        out_specs=pl.BlockSpec((1, 2 * size, LOOKS), lambda i: (i, 0, 0)),
        out_shape=jax.ShapeDtypeStruct((count, 2 * size, LOOKS), jnp.bfloat16),
        scratch_shapes=[pltpu.VMEM((size, width), jnp.float32)] * 2,
    )(same, cross, steer_re, steer_im)


def hermitian_parts(upper):
    def piece(left_pos, right_pos):
        start = block_pairs.index((left_pos, right_pos)) * 2 * CH
        return upper[:, :, start : start + 2 * CH]

    def real_block(left_pos, right_pos):
        if left_pos > right_pos:
            return jnp.swapaxes(real_block(right_pos, left_pos), 1, 2)
        return piece(left_pos, right_pos)[..., :CH]

    def imag_block(left_pos, right_pos):
        if left_pos > right_pos:
            return -jnp.swapaxes(imag_block(right_pos, left_pos), 1, 2)
        return -piece(left_pos, right_pos)[..., CH:]

    def assemble(block):
        rows = [jnp.concatenate([block(b, c) for c in range(3)], -1) for b in range(3)]
        return jnp.concatenate(rows, 1)

    return assemble(real_block), assemble(imag_block)


def body(echoes, training, look_index):
    spectra = doppler_spectra(echoes, twiddles())
    turned = lax.all_to_all(spectra, "dop", split_axis=0, concat_axis=1, tiled=True)
    turned = turned.reshape(turned.shape[0], -1, 2 * CH)
    edged = padded(turned, (("dop", 0),), 1)
    bin_count = edged.shape[0] - 2
    upper = upper_blocks(edged, training.astype(jnp.bfloat16))
    my_upper = sum_at_owner(upper, "rng", 0)
    my_unit = unit_vectors(*hermitian_parts(my_upper), steering(look_index))
    unit = gather_directly(my_unit, "rng", 0)
    shaped = unit.reshape(bin_count, 3, 2, CH, LOOKS)
    rotated = jnp.stack([-shaped[:, :, 1], shaped[:, :, 0]], axis=2).reshape(bin_count, SNAP, LOOKS)
    weights = jnp.concatenate([unit, rotated], axis=2)
    summed = None
    for position in range(3):
        term = jnp.einsum(
            "knj,krn->kjr",
            weights[:, position * 2 * CH : (position + 1) * 2 * CH],
            edged[position : position + bin_count],
            preferred_element_type=jnp.float32,
        )
        summed = term if summed is None else summed + term
    return summed.reshape(bin_count, 2, LOOKS, edged.shape[1])


def solution(mesh):
    in_specs = (P(("rng", "dop"), None, None, None), P("dop", "rng"), P())
    out_specs = P("dop", None, None, "rng")
    return jax.shard_map(body, mesh=mesh, in_specs=in_specs, out_specs=out_specs, check_vma=False)
```

```python
import jax
import jax.numpy as jnp
from jax import lax
from jax.sharding import PartitionSpec as P
from jax.experimental import pallas as pl
from jax.experimental.pallas import tpu as pltpu

CH = 32
PULSES = 128
LOOKS = 64
ANGLES = 256
SNAP = 192


loading = 0.1
epsilon = 1e-06
block_pairs = ((0, 0), (0, 1), (0, 2), (1, 1), (1, 2), (2, 2))


def padded(block, sides, width):
    for axis, dim in sides:
        count = lax.axis_size(axis)
        forward = [(i, i + 1) for i in range(count - 1)]
        forward.append((count - 1, 0))
        backward = [(target, source) for source, target in forward]
        low = lax.ppermute(
            lax.slice_in_dim(block, block.shape[dim] - width, None, axis=dim), axis, forward
        )
        high = lax.ppermute(lax.slice_in_dim(block, 0, width, axis=dim), axis, backward)
        block = jnp.concatenate([low, block, high], axis=dim)
    return block


def split_up(array, dim, count):
    dims = array.shape
    blocks = array.reshape(*dims[:dim], count, dims[dim] // count, *dims[dim + 1 :])
    return jnp.moveaxis(blocks, dim, 0)


def sum_at_owner(array, axis, dim):
    blocks = split_up(array, dim, lax.axis_size(axis))
    arrived = lax.all_to_all(blocks, axis, split_axis=0, concat_axis=0, tiled=True)
    return arrived.sum(axis=0)


def in_order(blocks, dim):
    dims = list(blocks.shape[1:])
    dims[dim] *= blocks.shape[0]
    return jnp.moveaxis(blocks, 0, dim).reshape(dims)


def copy_for_each(array, axis):
    count = lax.axis_size(axis)
    return lax.all_to_all(
        jnp.broadcast_to(array[None], (count, *array.shape)), axis, 0, 0, tiled=True
    )


def gather_directly(array, axis, dim):
    return in_order(copy_for_each(array, axis), dim)


def twiddles():
    pulse_ids = jnp.arange(PULSES, dtype=jnp.int32)
    phase_ids = pulse_ids[:, None] * pulse_ids[None, :] % PULSES
    angles = phase_ids.astype(jnp.float32) * (2.0 * jnp.pi / PULSES)
    return jnp.concatenate([jnp.cos(angles), jnp.sin(angles)], axis=0).astype(jnp.bfloat16)


def transform(twiddle_ref, echo_ref, out_ref):
    rows = echo_ref.shape[0]
    echoes = echo_ref[...]
    swapped = jnp.stack([echoes[:, 1], -echoes[:, 0]], axis=1)
    stacked = jnp.concatenate(
        [echoes.reshape(rows * 2 * CH, PULSES), swapped.reshape(rows * 2 * CH, PULSES)], axis=1
    )
    out_ref[...] = lax.dot_general(
        twiddle_ref[...], stacked, (((1,), (1,)), ((), ())), preferred_element_type=jnp.float32
    ).astype(out_ref.dtype)

def doppler_spectra(echo_rows, twiddle):
    rows = echo_rows.shape[0]
    paired = jnp.concatenate([twiddle[:PULSES], twiddle[PULSES:]], axis=1)
    return pl.pallas_call(
        transform,
        out_shape=jax.ShapeDtypeStruct((PULSES, rows * 2 * CH), jnp.bfloat16),
    )(paired, echo_rows)

def steering(look_index):
    sines = -1.0 + (2.0 * look_index.astype(jnp.float32) + 1.0) / ANGLES
    channel_ids = jnp.arange(CH).astype(jnp.float32)
    phases = jnp.pi * channel_ids[:, None] * sines[None, :]
    zeros = jnp.zeros((CH, LOOKS), jnp.float32)
    return jnp.stack([zeros, zeros, jnp.cos(phases), jnp.sin(phases), zeros, zeros]).reshape(
        SNAP, LOOKS
    )


def rotate(values):
    return jnp.concatenate([-values[..., CH:], values[..., :CH]], axis=-1)


def upper_blocks(edged, mask_rows):
    bin_count = edged.shape[0] - 2
    rotated = rotate(edged)
    snap = jnp.concatenate([edged[b : b + bin_count] for b in range(3)], axis=-1)
    turned_snap = jnp.concatenate([rotated[b : b + bin_count] for b in range(3)], axis=-1)
    both = jnp.concatenate([snap, turned_snap], axis=1)
    weighting = jnp.concatenate([mask_rows, mask_rows], axis=1)[:, :, None]
    masked = both * weighting
    leading = masked.reshape(*masked.shape[:2], 3, 2, CH)[:, :, :, 0].reshape(*masked.shape[:2], 3 * CH)
    rows = jnp.einsum("krn,krm->knm", leading, both, preferred_element_type=jnp.float32)
    pieces = [rows[:, b * CH : (b + 1) * CH, b * 2 * CH :] for b in range(3)]
    return jnp.concatenate(pieces, axis=-1)


def eliminate(real_ref, imag_ref, steer_re_ref, steer_im_ref, unit_ref, wr_ref, wi_ref):
    rows, cols = wr_ref.shape
    gap = cols - LOOKS
    lane_ids = lax.broadcasted_iota(jnp.int32, (1, cols), 1)
    row_ids = lax.broadcasted_iota(jnp.int32, (rows, 1), 0)
    diagonal = row_ids == lax.broadcasted_iota(jnp.int32, (1, rows), 1)
    same = real_ref[0]
    power = 2.0 * jnp.sum(jnp.where(diagonal, same, 0.0)) / SNAP + epsilon
    steer_re = steer_re_ref[...]
    steer_im = steer_im_ref[...]
    wr_ref[...] = jnp.zeros(wr_ref.shape, jnp.float32)
    wi_ref[...] = jnp.zeros(wi_ref.shape, jnp.float32)
    wr_ref[:, :rows] = same / power + jnp.where(diagonal, loading, 0.0)
    wi_ref[:, :rows] = imag_ref[0] / power
    wr_ref[:, gap:] = steer_re
    wi_ref[:, gap:] = steer_im

    def pick(values, hit):
        return jnp.sum(jnp.where(hit, values, 0.0), axis=1, keepdims=True)

    def times(a_r, a_i, b_r, b_i):
        return a_r * b_r - a_i * b_i, a_r * b_i + a_i * b_r

    def step(half, carry):
        j = 2 * half
        cur_r = wr_ref[...]
        cur_i = wi_ref[...]
        top_r = wr_ref[pl.ds(j, 1), :]
        top_i = wi_ref[pl.ds(j, 1), :]
        low_r = wr_ref[pl.ds(j + 1, 1), :]
        low_i = wi_ref[pl.ds(j + 1, 1), :]
        first = lane_ids == j
        second = lane_ids == j + 1
        a_r, a_i = pick(top_r, first), pick(top_i, first)
        b_r, b_i = pick(top_r, second), pick(top_i, second)
        c_r, c_i = pick(low_r, first), pick(low_i, first)
        d_r, d_i = pick(low_r, second), pick(low_i, second)
        ad_r, ad_i = times(a_r, a_i, d_r, d_i)
        bc_r, bc_i = times(b_r, b_i, c_r, c_i)
        det_r, det_i = ad_r - bc_r, ad_i - bc_i
        scale = 1.0 / (det_r * det_r + det_i * det_i)
        inv_r, inv_i = det_r * scale, -det_i * scale
        p_r, p_i = times(d_r, d_i, top_r, top_i)
        q_r, q_i = times(b_r, b_i, low_r, low_i)
        one_r, one_i = times(inv_r, inv_i, p_r - q_r, p_i - q_i)
        s_r, s_i = times(a_r, a_i, low_r, low_i)
        t_r, t_i = times(c_r, c_i, top_r, top_i)
        two_r, two_i = times(inv_r, inv_i, s_r - t_r, s_i - t_i)
        u_r, u_i = pick(cur_r, first), pick(cur_i, first)
        v_r, v_i = pick(cur_r, second), pick(cur_i, second)
        x_r, x_i = times(u_r, u_i, one_r, one_i)
        y_r, y_i = times(v_r, v_i, two_r, two_i)
        wr_ref[...] = cur_r - (x_r + y_r)
        wi_ref[...] = cur_i - (x_i + y_i)
        wr_ref[pl.ds(j, 1), :] = one_r
        wi_ref[pl.ds(j, 1), :] = one_i
        wr_ref[pl.ds(j + 1, 1), :] = two_r
        wi_ref[pl.ds(j + 1, 1), :] = two_i
        return carry

    lax.fori_loop(0, rows // 2, step, 0)
    solved_re = wr_ref[:, gap:]
    solved_im = wi_ref[:, gap:]
    root = jnp.sqrt(jnp.sum(steer_re * solved_re + steer_im * solved_im, axis=0, keepdims=True))
    unit_re = (solved_re / root).astype(unit_ref.dtype)
    unit_im = (solved_im / root).astype(unit_ref.dtype)
    for pos in range(rows // CH):
        unit_ref[0, 2 * pos * CH : (2 * pos + 1) * CH, :] = unit_re[pos * CH : (pos + 1) * CH]
        unit_ref[0, (2 * pos + 1) * CH : (2 * pos + 2) * CH, :] = unit_im[pos * CH : (pos + 1) * CH]

def unit_vectors(same, cross, steer):
    count, size, _ = same.shape
    parts = steer.reshape(size // CH, 2, CH, LOOKS)
    steer_re = parts[:, 0].reshape(size, LOOKS)
    steer_im = parts[:, 1].reshape(size, LOOKS)
    width = ((size + 127) // 128) * 128 + LOOKS
    matrix = pl.BlockSpec((1, size, size), lambda i: (i, 0, 0))
    vector = pl.BlockSpec((size, LOOKS), lambda i: (0, 0))
    return pl.pallas_call(
        eliminate,
        grid=(count,),
        in_specs=[matrix, matrix, vector, vector],
        out_specs=pl.BlockSpec((1, 2 * size, LOOKS), lambda i: (i, 0, 0)),
        out_shape=jax.ShapeDtypeStruct((count, 2 * size, LOOKS), jnp.bfloat16),
        scratch_shapes=[pltpu.VMEM((size, width), jnp.float32)] * 2,
    )(same, cross, steer_re, steer_im)


def hermitian_parts(upper):
    def piece(left_pos, right_pos):
        start = block_pairs.index((left_pos, right_pos)) * 2 * CH
        return upper[:, :, start : start + 2 * CH]

    def real_block(left_pos, right_pos):
        if left_pos > right_pos:
            return jnp.swapaxes(real_block(right_pos, left_pos), 1, 2)
        return piece(left_pos, right_pos)[..., :CH]

    def imag_block(left_pos, right_pos):
        if left_pos > right_pos:
            return -jnp.swapaxes(imag_block(right_pos, left_pos), 1, 2)
        return -piece(left_pos, right_pos)[..., CH:]

    def assemble(block):
        rows = [jnp.concatenate([block(b, c) for c in range(3)], -1) for b in range(3)]
        return jnp.concatenate(rows, 1)

    return assemble(real_block), assemble(imag_block)


def body(echoes, training, look_index):
    spectra = doppler_spectra(echoes, twiddles())
    turned = lax.all_to_all(spectra, "dop", split_axis=0, concat_axis=1, tiled=True)
    turned = turned.reshape(turned.shape[0], -1, 2 * CH)
    edged = padded(turned, (("dop", 0),), 1)
    bin_count = edged.shape[0] - 2
    upper = upper_blocks(edged, training.astype(jnp.bfloat16))
    my_upper = sum_at_owner(upper, "rng", 0)
    my_unit = unit_vectors(*hermitian_parts(my_upper), steering(look_index))
    unit = gather_directly(my_unit, "rng", 0)
    shaped = unit.reshape(bin_count, 3, 2, CH, LOOKS)
    rotated = jnp.stack([-shaped[:, :, 1], shaped[:, :, 0]], axis=2).reshape(bin_count, SNAP, LOOKS)
    weights = jnp.concatenate([unit, rotated], axis=2)
    summed = None
    for position in range(3):
        term = jnp.einsum(
            "knj,krn->kjr",
            weights[:, position * 2 * CH : (position + 1) * 2 * CH],
            edged[position : position + bin_count],
            preferred_element_type=jnp.float32,
        )
        summed = term if summed is None else summed + term
    return summed.reshape(bin_count, 2, LOOKS, edged.shape[1])


def solution(mesh):
    in_specs = (P(("rng", "dop"), None, None, None), P("dop", "rng"), P())
    out_specs = P("dop", None, None, "rng")
    return jax.shard_map(body, mesh=mesh, in_specs=in_specs, out_specs=out_specs, check_vma=False)
```

```python
import jax
import jax.numpy as jnp
from jax import lax
from jax.sharding import PartitionSpec as P
from jax.experimental import pallas as pl
from jax.experimental.pallas import tpu as pltpu

CH = 32
PULSES = 128
LOOKS = 64
ANGLES = 256
SNAP = 192


loading = 0.1
epsilon = 1e-06
block_pairs = ((0, 0), (0, 1), (0, 2), (1, 1), (1, 2), (2, 2))


def padded(block, sides, width):
    for axis, dim in sides:
        count = lax.axis_size(axis)
        forward = [(i, i + 1) for i in range(count - 1)]
        forward.append((count - 1, 0))
        backward = [(target, source) for source, target in forward]
        low = lax.ppermute(
            lax.slice_in_dim(block, block.shape[dim] - width, None, axis=dim), axis, forward
        )
        high = lax.ppermute(lax.slice_in_dim(block, 0, width, axis=dim), axis, backward)
        block = jnp.concatenate([low, block, high], axis=dim)
    return block


def split_up(array, dim, count):
    dims = array.shape
    blocks = array.reshape(*dims[:dim], count, dims[dim] // count, *dims[dim + 1 :])
    return jnp.moveaxis(blocks, dim, 0)


def sum_at_owner(array, axis, dim):
    blocks = split_up(array, dim, lax.axis_size(axis))
    arrived = lax.all_to_all(blocks, axis, split_axis=0, concat_axis=0, tiled=True)
    return arrived.sum(axis=0)


def in_order(blocks, dim):
    dims = list(blocks.shape[1:])
    dims[dim] *= blocks.shape[0]
    return jnp.moveaxis(blocks, 0, dim).reshape(dims)


def copy_for_each(array, axis):
    count = lax.axis_size(axis)
    return lax.all_to_all(
        jnp.broadcast_to(array[None], (count, *array.shape)), axis, 0, 0, tiled=True
    )


def gather_directly(array, axis, dim):
    return in_order(copy_for_each(array, axis), dim)


def twiddles():
    pulse_ids = jnp.arange(PULSES, dtype=jnp.int32)
    phase_ids = pulse_ids[:, None] * pulse_ids[None, :] % PULSES
    angles = phase_ids.astype(jnp.float32) * (2.0 * jnp.pi / PULSES)
    return jnp.concatenate([jnp.cos(angles), jnp.sin(angles)], axis=0).astype(jnp.bfloat16)


def transform(twiddle_ref, echo_ref, out_ref):
    rows = echo_ref.shape[0]
    echoes = echo_ref[...]
    swapped = jnp.stack([echoes[:, 1], -echoes[:, 0]], axis=1)
    stacked = jnp.concatenate(
        [echoes.reshape(rows * 2 * CH, PULSES), swapped.reshape(rows * 2 * CH, PULSES)], axis=1
    )
    out_ref[...] = lax.dot_general(
        twiddle_ref[...], stacked, (((1,), (1,)), ((), ())), preferred_element_type=jnp.float32
    ).astype(out_ref.dtype)

def doppler_spectra(echo_rows, twiddle):
    rows = echo_rows.shape[0]
    paired = jnp.concatenate([twiddle[:PULSES], twiddle[PULSES:]], axis=1)
    return pl.pallas_call(
        transform,
        out_shape=jax.ShapeDtypeStruct((PULSES, rows * 2 * CH), jnp.bfloat16),
    )(paired, echo_rows)

def steering(look_index):
    sines = -1.0 + (2.0 * look_index.astype(jnp.float32) + 1.0) / ANGLES
    channel_ids = jnp.arange(CH).astype(jnp.float32)
    phases = jnp.pi * channel_ids[:, None] * sines[None, :]
    zeros = jnp.zeros((CH, LOOKS), jnp.float32)
    return jnp.stack([zeros, zeros, jnp.cos(phases), jnp.sin(phases), zeros, zeros]).reshape(
        SNAP, LOOKS
    )


def rotate(values):
    return jnp.concatenate([-values[..., CH:], values[..., :CH]], axis=-1)


def upper_blocks(edged, mask_rows):
    bin_count = edged.shape[0] - 2
    rotated = rotate(edged)
    snap = jnp.concatenate([edged[b : b + bin_count] for b in range(3)], axis=-1)
    turned_snap = jnp.concatenate([rotated[b : b + bin_count] for b in range(3)], axis=-1)
    both = jnp.concatenate([snap, turned_snap], axis=1)
    weighting = jnp.concatenate([mask_rows, mask_rows], axis=1)[:, :, None]
    masked = both * weighting
    pieces = []
    for left_pos in range(3):
        pieces.append(
            jnp.einsum(
                "krn,krm->knm",
                masked[:, :, left_pos * 2 * CH : left_pos * 2 * CH + CH],
                both[:, :, left_pos * 2 * CH :],
                preferred_element_type=jnp.float32,
            )
        )
    return both[:, : edged.shape[1]], jnp.concatenate(pieces, axis=-1)


def eliminate(real_ref, imag_ref, steer_re_ref, steer_im_ref, unit_ref, wr_ref, wi_ref):
    rows, cols = wr_ref.shape
    gap = cols - LOOKS
    lane_ids = lax.broadcasted_iota(jnp.int32, (1, cols), 1)
    row_ids = lax.broadcasted_iota(jnp.int32, (rows, 1), 0)
    diagonal = row_ids == lax.broadcasted_iota(jnp.int32, (1, rows), 1)
    same = real_ref[0]
    power = 2.0 * jnp.sum(jnp.where(diagonal, same, 0.0)) / SNAP + epsilon
    steer_re = steer_re_ref[...]
    steer_im = steer_im_ref[...]
    wr_ref[...] = jnp.zeros(wr_ref.shape, jnp.float32)
    wi_ref[...] = jnp.zeros(wi_ref.shape, jnp.float32)
    wr_ref[:, :rows] = same / power + jnp.where(diagonal, loading, 0.0)
    wi_ref[:, :rows] = imag_ref[0] / power
    wr_ref[:, gap:] = steer_re
    wi_ref[:, gap:] = steer_im

    def pick(values, hit):
        return jnp.sum(jnp.where(hit, values, 0.0), axis=1, keepdims=True)

    def times(a_r, a_i, b_r, b_i):
        return a_r * b_r - a_i * b_i, a_r * b_i + a_i * b_r

    def step(half, carry):
        j = 2 * half
        cur_r = wr_ref[...]
        cur_i = wi_ref[...]
        top_r = wr_ref[pl.ds(j, 1), :]
        top_i = wi_ref[pl.ds(j, 1), :]
        low_r = wr_ref[pl.ds(j + 1, 1), :]
        low_i = wi_ref[pl.ds(j + 1, 1), :]
        first = lane_ids == j
        second = lane_ids == j + 1
        a_r, a_i = pick(top_r, first), pick(top_i, first)
        b_r, b_i = pick(top_r, second), pick(top_i, second)
        c_r, c_i = pick(low_r, first), pick(low_i, first)
        d_r, d_i = pick(low_r, second), pick(low_i, second)
        ad_r, ad_i = times(a_r, a_i, d_r, d_i)
        bc_r, bc_i = times(b_r, b_i, c_r, c_i)
        det_r, det_i = ad_r - bc_r, ad_i - bc_i
        scale = 1.0 / (det_r * det_r + det_i * det_i)
        inv_r, inv_i = det_r * scale, -det_i * scale
        p_r, p_i = times(d_r, d_i, top_r, top_i)
        q_r, q_i = times(b_r, b_i, low_r, low_i)
        one_r, one_i = times(inv_r, inv_i, p_r - q_r, p_i - q_i)
        s_r, s_i = times(a_r, a_i, low_r, low_i)
        t_r, t_i = times(c_r, c_i, top_r, top_i)
        two_r, two_i = times(inv_r, inv_i, s_r - t_r, s_i - t_i)
        u_r, u_i = pick(cur_r, first), pick(cur_i, first)
        v_r, v_i = pick(cur_r, second), pick(cur_i, second)
        x_r, x_i = times(u_r, u_i, one_r, one_i)
        y_r, y_i = times(v_r, v_i, two_r, two_i)
        wr_ref[...] = cur_r - (x_r + y_r)
        wi_ref[...] = cur_i - (x_i + y_i)
        wr_ref[pl.ds(j, 1), :] = one_r
        wi_ref[pl.ds(j, 1), :] = one_i
        wr_ref[pl.ds(j + 1, 1), :] = two_r
        wi_ref[pl.ds(j + 1, 1), :] = two_i
        return carry

    lax.fori_loop(0, rows // 2, step, 0)
    solved_re = wr_ref[:, gap:]
    solved_im = wi_ref[:, gap:]
    root = jnp.sqrt(jnp.sum(steer_re * solved_re + steer_im * solved_im, axis=0, keepdims=True))
    unit_re = (solved_re / root).astype(unit_ref.dtype)
    unit_im = (solved_im / root).astype(unit_ref.dtype)
    for pos in range(rows // CH):
        unit_ref[0, 2 * pos * CH : (2 * pos + 1) * CH, :] = unit_re[pos * CH : (pos + 1) * CH]
        unit_ref[0, (2 * pos + 1) * CH : (2 * pos + 2) * CH, :] = unit_im[pos * CH : (pos + 1) * CH]

def unit_vectors(same, cross, steer):
    count, size, _ = same.shape
    parts = steer.reshape(size // CH, 2, CH, LOOKS)
    steer_re = parts[:, 0].reshape(size, LOOKS)
    steer_im = parts[:, 1].reshape(size, LOOKS)
    width = ((size + 127) // 128) * 128 + LOOKS
    matrix = pl.BlockSpec((1, size, size), lambda i: (i, 0, 0))
    vector = pl.BlockSpec((size, LOOKS), lambda i: (0, 0))
    return pl.pallas_call(
        eliminate,
        grid=(count,),
        in_specs=[matrix, matrix, vector, vector],
        out_specs=pl.BlockSpec((1, 2 * size, LOOKS), lambda i: (i, 0, 0)),
        out_shape=jax.ShapeDtypeStruct((count, 2 * size, LOOKS), jnp.bfloat16),
        scratch_shapes=[pltpu.VMEM((size, width), jnp.float32)] * 2,
    )(same, cross, steer_re, steer_im)


def hermitian_parts(upper):
    def piece(left_pos, right_pos):
        start = block_pairs.index((left_pos, right_pos)) * 2 * CH
        return upper[:, :, start : start + 2 * CH]

    def real_block(left_pos, right_pos):
        if left_pos > right_pos:
            return jnp.swapaxes(real_block(right_pos, left_pos), 1, 2)
        return piece(left_pos, right_pos)[..., :CH]

    def imag_block(left_pos, right_pos):
        if left_pos > right_pos:
            return -jnp.swapaxes(imag_block(right_pos, left_pos), 1, 2)
        return -piece(left_pos, right_pos)[..., CH:]

    def assemble(block):
        rows = [jnp.concatenate([block(b, c) for c in range(3)], -1) for b in range(3)]
        return jnp.concatenate(rows, 1)

    return assemble(real_block), assemble(imag_block)


def body(echoes, training, look_index):
    spectra = doppler_spectra(echoes, twiddles())
    turned = lax.all_to_all(spectra, "dop", split_axis=0, concat_axis=1, tiled=True)
    turned = turned.reshape(turned.shape[0], -1, 2 * CH)
    edged = padded(turned, (("dop", 0),), 1)
    bin_count = edged.shape[0] - 2
    snap, upper = upper_blocks(edged, training.astype(jnp.bfloat16))
    my_upper = sum_at_owner(upper, "rng", 0)
    my_unit = unit_vectors(*hermitian_parts(my_upper), steering(look_index))
    unit = gather_directly(my_unit, "rng", 0)
    shaped = unit.reshape(bin_count, 3, 2, CH, LOOKS)
    rotated = jnp.stack([-shaped[:, :, 1], shaped[:, :, 0]], axis=2).reshape(bin_count, SNAP, LOOKS)
    weights = jnp.concatenate([unit, rotated], axis=2)
    summed = jnp.einsum("knj,krn->kjr", weights, snap, preferred_element_type=jnp.float32)
    return summed.reshape(bin_count, 2, LOOKS, edged.shape[1])


def solution(mesh):
    in_specs = (P(("rng", "dop"), None, None, None), P("dop", "rng"), P())
    out_specs = P("dop", None, None, "rng")
    return jax.shard_map(body, mesh=mesh, in_specs=in_specs, out_specs=out_specs, check_vma=False)
```

```python
import jax
import jax.numpy as jnp
from jax import lax
from jax.sharding import PartitionSpec as P
from jax.experimental import pallas as pl
from jax.experimental.pallas import tpu as pltpu

CH = 32
PULSES = 128
LOOKS = 64
ANGLES = 256
SNAP = 192


loading = 0.1
epsilon = 1e-06
block_pairs = ((0, 0), (0, 1), (0, 2), (1, 1), (1, 2), (2, 2))


def padded(block, sides, width):
    for axis, dim in sides:
        count = lax.axis_size(axis)
        forward = [(i, i + 1) for i in range(count - 1)]
        forward.append((count - 1, 0))
        backward = [(target, source) for source, target in forward]
        low = lax.ppermute(
            lax.slice_in_dim(block, block.shape[dim] - width, None, axis=dim), axis, forward
        )
        high = lax.ppermute(lax.slice_in_dim(block, 0, width, axis=dim), axis, backward)
        block = jnp.concatenate([low, block, high], axis=dim)
    return block


def split_up(array, dim, count):
    dims = array.shape
    blocks = array.reshape(*dims[:dim], count, dims[dim] // count, *dims[dim + 1 :])
    return jnp.moveaxis(blocks, dim, 0)


def sum_at_owner(array, axis, dim):
    blocks = split_up(array, dim, lax.axis_size(axis))
    arrived = lax.all_to_all(blocks, axis, split_axis=0, concat_axis=0, tiled=True)
    return arrived.sum(axis=0)


def in_order(blocks, dim):
    dims = list(blocks.shape[1:])
    dims[dim] *= blocks.shape[0]
    return jnp.moveaxis(blocks, 0, dim).reshape(dims)


def copy_for_each(array, axis):
    count = lax.axis_size(axis)
    return lax.all_to_all(
        jnp.broadcast_to(array[None], (count, *array.shape)), axis, 0, 0, tiled=True
    )


def gather_directly(array, axis, dim):
    return in_order(copy_for_each(array, axis), dim)


def twiddles():
    pulse_ids = jnp.arange(PULSES, dtype=jnp.int32)
    phase_ids = pulse_ids[:, None] * pulse_ids[None, :] % PULSES
    angles = phase_ids.astype(jnp.float32) * (2.0 * jnp.pi / PULSES)
    return jnp.concatenate([jnp.cos(angles), jnp.sin(angles)], axis=0).astype(jnp.bfloat16)


def transform(twiddle_ref, echo_ref, out_ref):
    rows = echo_ref.shape[0]
    echoes = echo_ref[...]
    swapped = jnp.stack([echoes[:, 1], -echoes[:, 0]], axis=1)
    stacked = jnp.concatenate(
        [echoes.reshape(rows * 2 * CH, PULSES), swapped.reshape(rows * 2 * CH, PULSES)], axis=1
    )
    out_ref[...] = lax.dot_general(
        twiddle_ref[...], stacked, (((1,), (1,)), ((), ())), preferred_element_type=jnp.float32
    ).astype(out_ref.dtype)

def doppler_spectra(echo_rows, twiddle):
    rows = echo_rows.shape[0]
    paired = jnp.concatenate([twiddle[:PULSES], twiddle[PULSES:]], axis=1)
    chunks = 4 if rows % 32 == 0 else 1
    step = rows // chunks
    return pl.pallas_call(
        transform,
        grid=(chunks,),
        in_specs=[
            pl.BlockSpec(paired.shape, lambda i: (0, 0)),
            pl.BlockSpec((step, 2, CH, PULSES), lambda i: (i, 0, 0, 0)),
        ],
        out_specs=pl.BlockSpec((PULSES, step * 2 * CH), lambda i: (0, i)),
        out_shape=jax.ShapeDtypeStruct((PULSES, rows * 2 * CH), jnp.bfloat16),
    )(paired, echo_rows)

def steering(look_index):
    sines = -1.0 + (2.0 * look_index.astype(jnp.float32) + 1.0) / ANGLES
    channel_ids = jnp.arange(CH).astype(jnp.float32)
    phases = jnp.pi * channel_ids[:, None] * sines[None, :]
    zeros = jnp.zeros((CH, LOOKS), jnp.float32)
    return jnp.stack([zeros, zeros, jnp.cos(phases), jnp.sin(phases), zeros, zeros]).reshape(
        SNAP, LOOKS
    )


def rotate(values):
    return jnp.concatenate([-values[..., CH:], values[..., :CH]], axis=-1)


def upper_blocks(edged, mask_rows):
    bin_count = edged.shape[0] - 2
    rotated = rotate(edged)
    snap = jnp.concatenate([edged[b : b + bin_count] for b in range(3)], axis=-1)
    turned_snap = jnp.concatenate([rotated[b : b + bin_count] for b in range(3)], axis=-1)
    both = jnp.concatenate([snap, turned_snap], axis=1)
    weighting = jnp.concatenate([mask_rows, mask_rows], axis=1)[:, :, None]
    masked = both * weighting
    pieces = []
    for left_pos in range(3):
        pieces.append(
            jnp.einsum(
                "krn,krm->knm",
                masked[:, :, left_pos * 2 * CH : left_pos * 2 * CH + CH],
                both[:, :, left_pos * 2 * CH :],
                preferred_element_type=jnp.float32,
            )
        )
    return jnp.concatenate(pieces, axis=-1)


def eliminate(real_ref, imag_ref, steer_re_ref, steer_im_ref, unit_ref, wr_ref, wi_ref):
    rows, cols = wr_ref.shape
    gap = cols - LOOKS
    lane_ids = lax.broadcasted_iota(jnp.int32, (1, cols), 1)
    row_ids = lax.broadcasted_iota(jnp.int32, (rows, 1), 0)
    diagonal = row_ids == lax.broadcasted_iota(jnp.int32, (1, rows), 1)
    same = real_ref[0]
    power = 2.0 * jnp.sum(jnp.where(diagonal, same, 0.0)) / SNAP + epsilon
    steer_re = steer_re_ref[...]
    steer_im = steer_im_ref[...]
    wr_ref[...] = jnp.zeros(wr_ref.shape, jnp.float32)
    wi_ref[...] = jnp.zeros(wi_ref.shape, jnp.float32)
    wr_ref[:, :rows] = same / power + jnp.where(diagonal, loading, 0.0)
    wi_ref[:, :rows] = imag_ref[0] / power
    wr_ref[:, gap:] = steer_re
    wi_ref[:, gap:] = steer_im

    def pick(values, hit):
        return jnp.sum(jnp.where(hit, values, 0.0), axis=1, keepdims=True)

    def times(a_r, a_i, b_r, b_i):
        return a_r * b_r - a_i * b_i, a_r * b_i + a_i * b_r

    def step(half, carry):
        j = 2 * half
        cur_r = wr_ref[...]
        cur_i = wi_ref[...]
        top_r = wr_ref[pl.ds(j, 1), :]
        top_i = wi_ref[pl.ds(j, 1), :]
        low_r = wr_ref[pl.ds(j + 1, 1), :]
        low_i = wi_ref[pl.ds(j + 1, 1), :]
        first = lane_ids == j
        second = lane_ids == j + 1
        a_r, a_i = pick(top_r, first), pick(top_i, first)
        b_r, b_i = pick(top_r, second), pick(top_i, second)
        c_r, c_i = pick(low_r, first), pick(low_i, first)
        d_r, d_i = pick(low_r, second), pick(low_i, second)
        ad_r, ad_i = times(a_r, a_i, d_r, d_i)
        bc_r, bc_i = times(b_r, b_i, c_r, c_i)
        det_r, det_i = ad_r - bc_r, ad_i - bc_i
        scale = 1.0 / (det_r * det_r + det_i * det_i)
        inv_r, inv_i = det_r * scale, -det_i * scale
        p_r, p_i = times(d_r, d_i, top_r, top_i)
        q_r, q_i = times(b_r, b_i, low_r, low_i)
        one_r, one_i = times(inv_r, inv_i, p_r - q_r, p_i - q_i)
        s_r, s_i = times(a_r, a_i, low_r, low_i)
        t_r, t_i = times(c_r, c_i, top_r, top_i)
        two_r, two_i = times(inv_r, inv_i, s_r - t_r, s_i - t_i)
        u_r, u_i = pick(cur_r, first), pick(cur_i, first)
        v_r, v_i = pick(cur_r, second), pick(cur_i, second)
        x_r, x_i = times(u_r, u_i, one_r, one_i)
        y_r, y_i = times(v_r, v_i, two_r, two_i)
        wr_ref[...] = cur_r - (x_r + y_r)
        wi_ref[...] = cur_i - (x_i + y_i)
        wr_ref[pl.ds(j, 1), :] = one_r
        wi_ref[pl.ds(j, 1), :] = one_i
        wr_ref[pl.ds(j + 1, 1), :] = two_r
        wi_ref[pl.ds(j + 1, 1), :] = two_i
        return carry

    lax.fori_loop(0, rows // 2, step, 0)
    solved_re = wr_ref[:, gap:]
    solved_im = wi_ref[:, gap:]
    root = jnp.sqrt(jnp.sum(steer_re * solved_re + steer_im * solved_im, axis=0, keepdims=True))
    unit_re = (solved_re / root).astype(unit_ref.dtype)
    unit_im = (solved_im / root).astype(unit_ref.dtype)
    for pos in range(rows // CH):
        unit_ref[0, 2 * pos * CH : (2 * pos + 1) * CH, :] = unit_re[pos * CH : (pos + 1) * CH]
        unit_ref[0, (2 * pos + 1) * CH : (2 * pos + 2) * CH, :] = unit_im[pos * CH : (pos + 1) * CH]

def unit_vectors(same, cross, steer):
    count, size, _ = same.shape
    parts = steer.reshape(size // CH, 2, CH, LOOKS)
    steer_re = parts[:, 0].reshape(size, LOOKS)
    steer_im = parts[:, 1].reshape(size, LOOKS)
    width = ((size + 127) // 128) * 128 + LOOKS
    matrix = pl.BlockSpec((1, size, size), lambda i: (i, 0, 0))
    vector = pl.BlockSpec((size, LOOKS), lambda i: (0, 0))
    return pl.pallas_call(
        eliminate,
        grid=(count,),
        in_specs=[matrix, matrix, vector, vector],
        out_specs=pl.BlockSpec((1, 2 * size, LOOKS), lambda i: (i, 0, 0)),
        out_shape=jax.ShapeDtypeStruct((count, 2 * size, LOOKS), jnp.bfloat16),
        scratch_shapes=[pltpu.VMEM((size, width), jnp.float32)] * 2,
    )(same, cross, steer_re, steer_im)


def hermitian_parts(upper):
    def piece(left_pos, right_pos):
        start = block_pairs.index((left_pos, right_pos)) * 2 * CH
        return upper[:, :, start : start + 2 * CH]

    def real_block(left_pos, right_pos):
        if left_pos > right_pos:
            return jnp.swapaxes(real_block(right_pos, left_pos), 1, 2)
        return piece(left_pos, right_pos)[..., :CH]

    def imag_block(left_pos, right_pos):
        if left_pos > right_pos:
            return -jnp.swapaxes(imag_block(right_pos, left_pos), 1, 2)
        return -piece(left_pos, right_pos)[..., CH:]

    def assemble(block):
        rows = [jnp.concatenate([block(b, c) for c in range(3)], -1) for b in range(3)]
        return jnp.concatenate(rows, 1)

    return assemble(real_block), assemble(imag_block)


def body(echoes, training, look_index):
    spectra = doppler_spectra(echoes, twiddles())
    turned = lax.all_to_all(spectra, "dop", split_axis=0, concat_axis=1, tiled=True)
    turned = turned.reshape(turned.shape[0], -1, 2 * CH)
    edged = padded(turned, (("dop", 0),), 1)
    bin_count = edged.shape[0] - 2
    upper = upper_blocks(edged, training.astype(jnp.bfloat16))
    my_upper = sum_at_owner(upper, "rng", 0)
    my_unit = unit_vectors(*hermitian_parts(my_upper), steering(look_index))
    unit = gather_directly(my_unit, "rng", 0)
    shaped = unit.reshape(bin_count, 3, 2, CH, LOOKS)
    rotated = jnp.stack([-shaped[:, :, 1], shaped[:, :, 0]], axis=2).reshape(bin_count, SNAP, LOOKS)
    weights = jnp.concatenate([unit, rotated], axis=2)
    summed = None
    for position in range(3):
        term = jnp.einsum(
            "knj,krn->kjr",
            weights[:, position * 2 * CH : (position + 1) * 2 * CH],
            edged[position : position + bin_count],
            preferred_element_type=jnp.float32,
        )
        summed = term if summed is None else summed + term
    return summed.reshape(bin_count, 2, LOOKS, edged.shape[1])


def solution(mesh):
    in_specs = (P(("rng", "dop"), None, None, None), P("dop", "rng"), P())
    out_specs = P("dop", None, None, "rng")
    return jax.shard_map(body, mesh=mesh, in_specs=in_specs, out_specs=out_specs, check_vma=False)
```

```python
import jax
import jax.numpy as jnp
from jax import lax
from jax.sharding import PartitionSpec as P
from jax.experimental import pallas as pl
from jax.experimental.pallas import tpu as pltpu

CH = 32
PULSES = 128
LOOKS = 64
ANGLES = 256
SNAP = 192


loading = 0.1
epsilon = 1e-06
block_pairs = ((0, 0), (0, 1), (0, 2), (1, 1), (1, 2), (2, 2))


def padded(block, sides, width):
    for axis, dim in sides:
        count = lax.axis_size(axis)
        forward = [(i, i + 1) for i in range(count - 1)]
        forward.append((count - 1, 0))
        backward = [(target, source) for source, target in forward]
        low = lax.ppermute(
            lax.slice_in_dim(block, block.shape[dim] - width, None, axis=dim), axis, forward
        )
        high = lax.ppermute(lax.slice_in_dim(block, 0, width, axis=dim), axis, backward)
        block = jnp.concatenate([low, block, high], axis=dim)
    return block


def split_up(array, dim, count):
    dims = array.shape
    blocks = array.reshape(*dims[:dim], count, dims[dim] // count, *dims[dim + 1 :])
    return jnp.moveaxis(blocks, dim, 0)


def sum_at_owner(array, axis, dim):
    blocks = split_up(array, dim, lax.axis_size(axis))
    arrived = lax.all_to_all(blocks, axis, split_axis=0, concat_axis=0, tiled=True)
    return arrived.sum(axis=0)


def in_order(blocks, dim):
    dims = list(blocks.shape[1:])
    dims[dim] *= blocks.shape[0]
    return jnp.moveaxis(blocks, 0, dim).reshape(dims)


def copy_for_each(array, axis):
    count = lax.axis_size(axis)
    return lax.all_to_all(
        jnp.broadcast_to(array[None], (count, *array.shape)), axis, 0, 0, tiled=True
    )


def gather_directly(array, axis, dim):
    return in_order(copy_for_each(array, axis), dim)


def twiddles():
    pulse_ids = jnp.arange(PULSES, dtype=jnp.int32)
    phase_ids = pulse_ids[:, None] * pulse_ids[None, :] % PULSES
    angles = phase_ids.astype(jnp.float32) * (2.0 * jnp.pi / PULSES)
    return jnp.concatenate([jnp.cos(angles), jnp.sin(angles)], axis=0).astype(jnp.bfloat16)


def transform(cosine_ref, sine_ref, echo_ref, out_ref):
    rows = echo_ref.shape[0]
    echoes = echo_ref[...]
    swapped = jnp.stack([echoes[:, 1], -echoes[:, 0]], axis=1)
    stacked = jnp.concatenate(
        [echoes.reshape(rows * 2 * CH, PULSES), swapped.reshape(rows * 2 * CH, PULSES)], axis=1
    )
    paired = jnp.concatenate([cosine_ref[...], sine_ref[...]], axis=1)
    out_ref[...] = lax.dot_general(
        paired, stacked, (((1,), (1,)), ((), ())), preferred_element_type=jnp.float32
    ).astype(out_ref.dtype)

def doppler_spectra(echo_rows, twiddle):
    rows = echo_rows.shape[0]
    return pl.pallas_call(
        transform,
        out_shape=jax.ShapeDtypeStruct((PULSES, rows * 2 * CH), jnp.bfloat16),
    )(twiddle[:PULSES], twiddle[PULSES:], echo_rows)

def steering(look_index):
    sines = -1.0 + (2.0 * look_index.astype(jnp.float32) + 1.0) / ANGLES
    channel_ids = jnp.arange(CH).astype(jnp.float32)
    phases = jnp.pi * channel_ids[:, None] * sines[None, :]
    zeros = jnp.zeros((CH, LOOKS), jnp.float32)
    return jnp.stack([zeros, zeros, jnp.cos(phases), jnp.sin(phases), zeros, zeros]).reshape(
        SNAP, LOOKS
    )


def rotate(values):
    return jnp.concatenate([-values[..., CH:], values[..., :CH]], axis=-1)


def upper_blocks(edged, mask_rows):
    bin_count = edged.shape[0] - 2
    rotated = rotate(edged)
    snap = jnp.concatenate([edged[b : b + bin_count] for b in range(3)], axis=-1)
    turned_snap = jnp.concatenate([rotated[b : b + bin_count] for b in range(3)], axis=-1)
    both = jnp.concatenate([snap, turned_snap], axis=1)
    weighting = jnp.concatenate([mask_rows, mask_rows], axis=1)[:, :, None]
    masked = both * weighting
    pieces = []
    for left_pos in range(3):
        pieces.append(
            jnp.einsum(
                "krn,krm->knm",
                masked[:, :, left_pos * 2 * CH : left_pos * 2 * CH + CH],
                both[:, :, left_pos * 2 * CH :],
                preferred_element_type=jnp.float32,
            )
        )
    return jnp.concatenate(pieces, axis=-1)


def eliminate(real_ref, imag_ref, steer_re_ref, steer_im_ref, unit_ref, wr_ref, wi_ref):
    rows, cols = wr_ref.shape
    gap = cols - LOOKS
    lane_ids = lax.broadcasted_iota(jnp.int32, (1, cols), 1)
    row_ids = lax.broadcasted_iota(jnp.int32, (rows, 1), 0)
    diagonal = row_ids == lax.broadcasted_iota(jnp.int32, (1, rows), 1)
    same = real_ref[0]
    power = 2.0 * jnp.sum(jnp.where(diagonal, same, 0.0)) / SNAP + epsilon
    steer_re = steer_re_ref[...]
    steer_im = steer_im_ref[...]
    wr_ref[...] = jnp.zeros(wr_ref.shape, jnp.float32)
    wi_ref[...] = jnp.zeros(wi_ref.shape, jnp.float32)
    wr_ref[:, :rows] = same / power + jnp.where(diagonal, loading, 0.0)
    wi_ref[:, :rows] = imag_ref[0] / power
    wr_ref[:, gap:] = steer_re
    wi_ref[:, gap:] = steer_im

    def pick(values, hit):
        return jnp.sum(jnp.where(hit, values, 0.0), axis=1, keepdims=True)

    def times(a_r, a_i, b_r, b_i):
        return a_r * b_r - a_i * b_i, a_r * b_i + a_i * b_r

    def step(half, carry):
        j = 2 * half
        cur_r = wr_ref[...]
        cur_i = wi_ref[...]
        top_r = wr_ref[pl.ds(j, 1), :]
        top_i = wi_ref[pl.ds(j, 1), :]
        low_r = wr_ref[pl.ds(j + 1, 1), :]
        low_i = wi_ref[pl.ds(j + 1, 1), :]
        first = lane_ids == j
        second = lane_ids == j + 1
        a_r, a_i = pick(top_r, first), pick(top_i, first)
        b_r, b_i = pick(top_r, second), pick(top_i, second)
        c_r, c_i = pick(low_r, first), pick(low_i, first)
        d_r, d_i = pick(low_r, second), pick(low_i, second)
        ad_r, ad_i = times(a_r, a_i, d_r, d_i)
        bc_r, bc_i = times(b_r, b_i, c_r, c_i)
        det_r, det_i = ad_r - bc_r, ad_i - bc_i
        scale = 1.0 / (det_r * det_r + det_i * det_i)
        inv_r, inv_i = det_r * scale, -det_i * scale
        p_r, p_i = times(d_r, d_i, top_r, top_i)
        q_r, q_i = times(b_r, b_i, low_r, low_i)
        one_r, one_i = times(inv_r, inv_i, p_r - q_r, p_i - q_i)
        s_r, s_i = times(a_r, a_i, low_r, low_i)
        t_r, t_i = times(c_r, c_i, top_r, top_i)
        two_r, two_i = times(inv_r, inv_i, s_r - t_r, s_i - t_i)
        u_r, u_i = pick(cur_r, first), pick(cur_i, first)
        v_r, v_i = pick(cur_r, second), pick(cur_i, second)
        x_r, x_i = times(u_r, u_i, one_r, one_i)
        y_r, y_i = times(v_r, v_i, two_r, two_i)
        wr_ref[...] = cur_r - (x_r + y_r)
        wi_ref[...] = cur_i - (x_i + y_i)
        wr_ref[pl.ds(j, 1), :] = one_r
        wi_ref[pl.ds(j, 1), :] = one_i
        wr_ref[pl.ds(j + 1, 1), :] = two_r
        wi_ref[pl.ds(j + 1, 1), :] = two_i
        return carry

    lax.fori_loop(0, rows // 2, step, 0)
    solved_re = wr_ref[:, gap:]
    solved_im = wi_ref[:, gap:]
    root = jnp.sqrt(jnp.sum(steer_re * solved_re + steer_im * solved_im, axis=0, keepdims=True))
    unit_re = (solved_re / root).astype(unit_ref.dtype)
    unit_im = (solved_im / root).astype(unit_ref.dtype)
    for pos in range(rows // CH):
        unit_ref[0, 2 * pos * CH : (2 * pos + 1) * CH, :] = unit_re[pos * CH : (pos + 1) * CH]
        unit_ref[0, (2 * pos + 1) * CH : (2 * pos + 2) * CH, :] = unit_im[pos * CH : (pos + 1) * CH]

def unit_vectors(same, cross, steer):
    count, size, _ = same.shape
    parts = steer.reshape(size // CH, 2, CH, LOOKS)
    steer_re = parts[:, 0].reshape(size, LOOKS)
    steer_im = parts[:, 1].reshape(size, LOOKS)
    width = ((size + 127) // 128) * 128 + LOOKS
    matrix = pl.BlockSpec((1, size, size), lambda i: (i, 0, 0))
    vector = pl.BlockSpec((size, LOOKS), lambda i: (0, 0))
    return pl.pallas_call(
        eliminate,
        grid=(count,),
        in_specs=[matrix, matrix, vector, vector],
        out_specs=pl.BlockSpec((1, 2 * size, LOOKS), lambda i: (i, 0, 0)),
        out_shape=jax.ShapeDtypeStruct((count, 2 * size, LOOKS), jnp.bfloat16),
        scratch_shapes=[pltpu.VMEM((size, width), jnp.float32)] * 2,
    )(same, cross, steer_re, steer_im)


def hermitian_parts(upper):
    def piece(left_pos, right_pos):
        start = block_pairs.index((left_pos, right_pos)) * 2 * CH
        return upper[:, :, start : start + 2 * CH]

    def real_block(left_pos, right_pos):
        if left_pos > right_pos:
            return jnp.swapaxes(real_block(right_pos, left_pos), 1, 2)
        return piece(left_pos, right_pos)[..., :CH]

    def imag_block(left_pos, right_pos):
        if left_pos > right_pos:
            return -jnp.swapaxes(imag_block(right_pos, left_pos), 1, 2)
        return -piece(left_pos, right_pos)[..., CH:]

    def assemble(block):
        rows = [jnp.concatenate([block(b, c) for c in range(3)], -1) for b in range(3)]
        return jnp.concatenate(rows, 1)

    return assemble(real_block), assemble(imag_block)


def body(echoes, training, look_index):
    spectra = doppler_spectra(echoes, twiddles())
    turned = lax.all_to_all(spectra, "dop", split_axis=0, concat_axis=1, tiled=True)
    turned = turned.reshape(turned.shape[0], -1, 2 * CH)
    edged = padded(turned, (("dop", 0),), 1)
    bin_count = edged.shape[0] - 2
    upper = upper_blocks(edged, training.astype(jnp.bfloat16))
    my_upper = sum_at_owner(upper, "rng", 0)
    my_unit = unit_vectors(*hermitian_parts(my_upper), steering(look_index))
    unit = gather_directly(my_unit, "rng", 0)
    shaped = unit.reshape(bin_count, 3, 2, CH, LOOKS)
    rotated = jnp.stack([-shaped[:, :, 1], shaped[:, :, 0]], axis=2).reshape(bin_count, SNAP, LOOKS)
    weights = jnp.concatenate([unit, rotated], axis=2)
    summed = None
    for position in range(3):
        term = jnp.einsum(
            "knj,krn->kjr",
            weights[:, position * 2 * CH : (position + 1) * 2 * CH],
            edged[position : position + bin_count],
            preferred_element_type=jnp.float32,
        )
        summed = term if summed is None else summed + term
    return summed.reshape(bin_count, 2, LOOKS, edged.shape[1])


def solution(mesh):
    in_specs = (P(("rng", "dop"), None, None, None), P("dop", "rng"), P())
    out_specs = P("dop", None, None, "rng")
    return jax.shard_map(body, mesh=mesh, in_specs=in_specs, out_specs=out_specs, check_vma=False)
```

```python
import jax
import jax.numpy as jnp
from jax import lax
from jax.sharding import PartitionSpec as P
from jax.experimental import pallas as pl
from jax.experimental.pallas import tpu as pltpu

CH = 32
PULSES = 128
LOOKS = 64
ANGLES = 256
SNAP = 192


loading = 0.1
epsilon = 1e-06
block_pairs = ((0, 0), (0, 1), (0, 2), (1, 1), (1, 2), (2, 2))


def padded(block, sides, width):
    for axis, dim in sides:
        count = lax.axis_size(axis)
        forward = [(i, i + 1) for i in range(count - 1)]
        forward.append((count - 1, 0))
        backward = [(target, source) for source, target in forward]
        low = lax.ppermute(
            lax.slice_in_dim(block, block.shape[dim] - width, None, axis=dim), axis, forward
        )
        high = lax.ppermute(lax.slice_in_dim(block, 0, width, axis=dim), axis, backward)
        block = jnp.concatenate([low, block, high], axis=dim)
    return block


def split_up(array, dim, count):
    dims = array.shape
    blocks = array.reshape(*dims[:dim], count, dims[dim] // count, *dims[dim + 1 :])
    return jnp.moveaxis(blocks, dim, 0)


def sum_at_owner(array, axis, dim):
    blocks = split_up(array, dim, lax.axis_size(axis))
    arrived = lax.all_to_all(blocks, axis, split_axis=0, concat_axis=0, tiled=True)
    return arrived.sum(axis=0)


def in_order(blocks, dim):
    dims = list(blocks.shape[1:])
    dims[dim] *= blocks.shape[0]
    return jnp.moveaxis(blocks, 0, dim).reshape(dims)


def copy_for_each(array, axis):
    count = lax.axis_size(axis)
    return lax.all_to_all(
        jnp.broadcast_to(array[None], (count, *array.shape)), axis, 0, 0, tiled=True
    )


def gather_directly(array, axis, dim):
    return in_order(copy_for_each(array, axis), dim)


def twiddles():
    pulse_ids = jnp.arange(PULSES, dtype=jnp.int32)
    phase_ids = pulse_ids[:, None] * pulse_ids[None, :] % PULSES
    angles = phase_ids.astype(jnp.float32) * (2.0 * jnp.pi / PULSES)
    return jnp.concatenate([jnp.cos(angles), jnp.sin(angles)], axis=0).astype(jnp.bfloat16)


def transform(cosine_ref, sine_ref, echo_ref, out_ref):
    rows = echo_ref.shape[0]
    echoes = echo_ref[...]
    swapped = jnp.stack([echoes[:, 1], -echoes[:, 0]], axis=1)
    stacked = jnp.concatenate(
        [echoes.reshape(rows * 2 * CH, PULSES), swapped.reshape(rows * 2 * CH, PULSES)], axis=1
    )
    paired = jnp.concatenate([cosine_ref[...], sine_ref[...]], axis=1)
    out_ref[...] = lax.dot_general(
        paired, stacked, (((1,), (1,)), ((), ())), preferred_element_type=jnp.float32
    ).astype(out_ref.dtype)

def doppler_spectra(echo_rows, twiddle):
    rows = echo_rows.shape[0]
    return pl.pallas_call(
        transform,
        out_shape=jax.ShapeDtypeStruct((PULSES, rows * 2 * CH), jnp.bfloat16),
    )(twiddle[:PULSES], twiddle[PULSES:], echo_rows)

def steering(look_index):
    sines = -1.0 + (2.0 * look_index.astype(jnp.float32) + 1.0) / ANGLES
    channel_ids = jnp.arange(CH).astype(jnp.float32)
    phases = jnp.pi * channel_ids[:, None] * sines[None, :]
    zeros = jnp.zeros((CH, LOOKS), jnp.float32)
    return jnp.stack([zeros, zeros, jnp.cos(phases), jnp.sin(phases), zeros, zeros]).reshape(
        SNAP, LOOKS
    )


def rotate(values):
    return jnp.concatenate([-values[..., CH:], values[..., :CH]], axis=-1)


def upper_blocks(edged, mask_rows):
    bin_count = edged.shape[0] - 2
    rotated = rotate(edged)
    snap = jnp.concatenate([edged[b : b + bin_count] for b in range(3)], axis=-1)
    turned_snap = jnp.concatenate([rotated[b : b + bin_count] for b in range(3)], axis=-1)
    both = jnp.concatenate([snap, turned_snap], axis=1)
    weighting = jnp.concatenate([mask_rows, mask_rows], axis=1)[:, :, None]
    masked = both * weighting
    pieces = []
    for left_pos in range(3):
        pieces.append(
            jnp.einsum(
                "krn,krm->knm",
                masked[:, :, left_pos * 2 * CH : left_pos * 2 * CH + CH],
                both[:, :, left_pos * 2 * CH :],
                preferred_element_type=jnp.float32,
            )
        )
    return jnp.concatenate(pieces, axis=-1)


def eliminate(parts_ref, steer_re_ref, steer_im_ref, unit_ref, wr_ref, wi_ref):
    rows, cols = wr_ref.shape
    gap = cols - LOOKS
    lane_ids = lax.broadcasted_iota(jnp.int32, (1, cols), 1)
    row_ids = lax.broadcasted_iota(jnp.int32, (rows, 1), 0)
    diagonal = row_ids == lax.broadcasted_iota(jnp.int32, (1, rows), 1)
    same = parts_ref[0, 0]
    power = 2.0 * jnp.sum(jnp.where(diagonal, same, 0.0)) / SNAP + epsilon
    steer_re = steer_re_ref[...]
    steer_im = steer_im_ref[...]
    wr_ref[...] = jnp.zeros(wr_ref.shape, jnp.float32)
    wi_ref[...] = jnp.zeros(wi_ref.shape, jnp.float32)
    wr_ref[:, :rows] = same / power + jnp.where(diagonal, loading, 0.0)
    wi_ref[:, :rows] = parts_ref[0, 1] / power
    wr_ref[:, gap:] = steer_re
    wi_ref[:, gap:] = steer_im

    def pick(values, hit):
        return jnp.sum(jnp.where(hit, values, 0.0), axis=1, keepdims=True)

    def times(a_r, a_i, b_r, b_i):
        return a_r * b_r - a_i * b_i, a_r * b_i + a_i * b_r

    def step(half, carry):
        j = 2 * half
        cur_r = wr_ref[...]
        cur_i = wi_ref[...]
        top_r = wr_ref[pl.ds(j, 1), :]
        top_i = wi_ref[pl.ds(j, 1), :]
        low_r = wr_ref[pl.ds(j + 1, 1), :]
        low_i = wi_ref[pl.ds(j + 1, 1), :]
        first = lane_ids == j
        second = lane_ids == j + 1
        a_r, a_i = pick(top_r, first), pick(top_i, first)
        b_r, b_i = pick(top_r, second), pick(top_i, second)
        c_r, c_i = pick(low_r, first), pick(low_i, first)
        d_r, d_i = pick(low_r, second), pick(low_i, second)
        ad_r, ad_i = times(a_r, a_i, d_r, d_i)
        bc_r, bc_i = times(b_r, b_i, c_r, c_i)
        det_r, det_i = ad_r - bc_r, ad_i - bc_i
        scale = 1.0 / (det_r * det_r + det_i * det_i)
        inv_r, inv_i = det_r * scale, -det_i * scale
        p_r, p_i = times(d_r, d_i, top_r, top_i)
        q_r, q_i = times(b_r, b_i, low_r, low_i)
        one_r, one_i = times(inv_r, inv_i, p_r - q_r, p_i - q_i)
        s_r, s_i = times(a_r, a_i, low_r, low_i)
        t_r, t_i = times(c_r, c_i, top_r, top_i)
        two_r, two_i = times(inv_r, inv_i, s_r - t_r, s_i - t_i)
        u_r, u_i = pick(cur_r, first), pick(cur_i, first)
        v_r, v_i = pick(cur_r, second), pick(cur_i, second)
        x_r, x_i = times(u_r, u_i, one_r, one_i)
        y_r, y_i = times(v_r, v_i, two_r, two_i)
        wr_ref[...] = cur_r - (x_r + y_r)
        wi_ref[...] = cur_i - (x_i + y_i)
        wr_ref[pl.ds(j, 1), :] = one_r
        wi_ref[pl.ds(j, 1), :] = one_i
        wr_ref[pl.ds(j + 1, 1), :] = two_r
        wi_ref[pl.ds(j + 1, 1), :] = two_i
        return carry

    lax.fori_loop(0, rows // 2, step, 0)
    solved_re = wr_ref[:, gap:]
    solved_im = wi_ref[:, gap:]
    root = jnp.sqrt(jnp.sum(steer_re * solved_re + steer_im * solved_im, axis=0, keepdims=True))
    unit_re = (solved_re / root).astype(unit_ref.dtype)
    unit_im = (solved_im / root).astype(unit_ref.dtype)
    for pos in range(rows // CH):
        unit_ref[0, 2 * pos * CH : (2 * pos + 1) * CH, :] = unit_re[pos * CH : (pos + 1) * CH]
        unit_ref[0, (2 * pos + 1) * CH : (2 * pos + 2) * CH, :] = unit_im[pos * CH : (pos + 1) * CH]

def unit_vectors(same, cross, steer):
    count, size, _ = same.shape
    parts = jnp.stack([same, cross], axis=1)
    halves = steer.reshape(size // CH, 2, CH, LOOKS)
    steer_re = halves[:, 0].reshape(size, LOOKS)
    steer_im = halves[:, 1].reshape(size, LOOKS)
    width = ((size + 127) // 128) * 128 + LOOKS
    vector = pl.BlockSpec((size, LOOKS), lambda i: (0, 0))
    return pl.pallas_call(
        eliminate,
        grid=(count,),
        in_specs=[pl.BlockSpec((1, 2, size, size), lambda i: (i, 0, 0, 0)), vector, vector],
        out_specs=pl.BlockSpec((1, 2 * size, LOOKS), lambda i: (i, 0, 0)),
        out_shape=jax.ShapeDtypeStruct((count, 2 * size, LOOKS), jnp.bfloat16),
        scratch_shapes=[pltpu.VMEM((size, width), jnp.float32)] * 2,
    )(parts, steer_re, steer_im)


def hermitian_parts(upper):
    def piece(left_pos, right_pos):
        start = block_pairs.index((left_pos, right_pos)) * 2 * CH
        return upper[:, :, start : start + 2 * CH]

    def real_block(left_pos, right_pos):
        if left_pos > right_pos:
            return jnp.swapaxes(real_block(right_pos, left_pos), 1, 2)
        return piece(left_pos, right_pos)[..., :CH]

    def imag_block(left_pos, right_pos):
        if left_pos > right_pos:
            return -jnp.swapaxes(imag_block(right_pos, left_pos), 1, 2)
        return -piece(left_pos, right_pos)[..., CH:]

    def assemble(block):
        rows = [jnp.concatenate([block(b, c) for c in range(3)], -1) for b in range(3)]
        return jnp.concatenate(rows, 1)

    return assemble(real_block), assemble(imag_block)


def body(echoes, training, look_index):
    spectra = doppler_spectra(echoes, twiddles())
    turned = lax.all_to_all(spectra, "dop", split_axis=0, concat_axis=1, tiled=True)
    turned = turned.reshape(turned.shape[0], -1, 2 * CH)
    edged = padded(turned, (("dop", 0),), 1)
    bin_count = edged.shape[0] - 2
    upper = upper_blocks(edged, training.astype(jnp.bfloat16))
    my_upper = sum_at_owner(upper, "rng", 0)
    my_unit = unit_vectors(*hermitian_parts(my_upper), steering(look_index))
    unit = gather_directly(my_unit, "rng", 0)
    shaped = unit.reshape(bin_count, 3, 2, CH, LOOKS)
    rotated = jnp.stack([-shaped[:, :, 1], shaped[:, :, 0]], axis=2).reshape(bin_count, SNAP, LOOKS)
    weights = jnp.concatenate([unit, rotated], axis=2)
    summed = None
    for position in range(3):
        term = jnp.einsum(
            "knj,krn->kjr",
            weights[:, position * 2 * CH : (position + 1) * 2 * CH],
            edged[position : position + bin_count],
            preferred_element_type=jnp.float32,
        )
        summed = term if summed is None else summed + term
    return summed.reshape(bin_count, 2, LOOKS, edged.shape[1])


def solution(mesh):
    in_specs = (P(("rng", "dop"), None, None, None), P("dop", "rng"), P())
    out_specs = P("dop", None, None, "rng")
    return jax.shard_map(body, mesh=mesh, in_specs=in_specs, out_specs=out_specs, check_vma=False)
```

```python
import jax
import jax.numpy as jnp
from jax import lax
from jax.sharding import PartitionSpec as P
from jax.experimental import pallas as pl
from jax.experimental.pallas import tpu as pltpu

CH = 32
PULSES = 128
LOOKS = 64
ANGLES = 256
SNAP = 192


loading = 0.1
epsilon = 1e-06
block_pairs = ((0, 0), (0, 1), (0, 2), (1, 1), (1, 2), (2, 2))


def padded(block, sides, width):
    for axis, dim in sides:
        count = lax.axis_size(axis)
        forward = [(i, i + 1) for i in range(count - 1)]
        forward.append((count - 1, 0))
        backward = [(target, source) for source, target in forward]
        low = lax.ppermute(
            lax.slice_in_dim(block, block.shape[dim] - width, None, axis=dim), axis, forward
        )
        high = lax.ppermute(lax.slice_in_dim(block, 0, width, axis=dim), axis, backward)
        block = jnp.concatenate([low, block, high], axis=dim)
    return block


def split_up(array, dim, count):
    dims = array.shape
    blocks = array.reshape(*dims[:dim], count, dims[dim] // count, *dims[dim + 1 :])
    return jnp.moveaxis(blocks, dim, 0)


def sum_at_owner(array, axis, dim):
    blocks = split_up(array, dim, lax.axis_size(axis))
    arrived = lax.all_to_all(blocks, axis, split_axis=0, concat_axis=0, tiled=True)
    return arrived.sum(axis=0)


def in_order(blocks, dim):
    dims = list(blocks.shape[1:])
    dims[dim] *= blocks.shape[0]
    return jnp.moveaxis(blocks, 0, dim).reshape(dims)


def copy_for_each(array, axis):
    count = lax.axis_size(axis)
    return lax.all_to_all(
        jnp.broadcast_to(array[None], (count, *array.shape)), axis, 0, 0, tiled=True
    )


def gather_directly(array, axis, dim):
    return in_order(copy_for_each(array, axis), dim)


def twiddles():
    pulse_ids = jnp.arange(PULSES, dtype=jnp.int32)
    phase_ids = pulse_ids[:, None] * pulse_ids[None, :] % PULSES
    angles = phase_ids.astype(jnp.float32) * (2.0 * jnp.pi / PULSES)
    return jnp.concatenate([jnp.cos(angles), jnp.sin(angles)], axis=0).astype(jnp.bfloat16)


def transform(cosine_ref, sine_ref, echo_ref, out_ref):
    rows = echo_ref.shape[0]
    echoes = echo_ref[...]
    swapped = jnp.stack([echoes[:, 1], -echoes[:, 0]], axis=1)
    stacked = jnp.concatenate(
        [echoes.reshape(rows * 2 * CH, PULSES), swapped.reshape(rows * 2 * CH, PULSES)], axis=1
    )
    paired = jnp.concatenate([cosine_ref[...], sine_ref[...]], axis=1)
    out_ref[...] = lax.dot_general(
        paired, stacked, (((1,), (1,)), ((), ())), preferred_element_type=jnp.float32
    ).astype(out_ref.dtype)

def doppler_spectra(echo_rows, twiddle):
    rows = echo_rows.shape[0]
    return pl.pallas_call(
        transform,
        out_shape=jax.ShapeDtypeStruct((PULSES, rows * 2 * CH), jnp.bfloat16),
    )(twiddle[:PULSES], twiddle[PULSES:], echo_rows)

def steering(look_index):
    sines = -1.0 + (2.0 * look_index.astype(jnp.float32) + 1.0) / ANGLES
    channel_ids = jnp.arange(CH).astype(jnp.float32)
    phases = jnp.pi * channel_ids[:, None] * sines[None, :]
    zeros = jnp.zeros((CH, LOOKS), jnp.float32)
    return jnp.stack([zeros, zeros, jnp.cos(phases), jnp.sin(phases), zeros, zeros]).reshape(
        SNAP, LOOKS
    )


def rotate(values):
    return jnp.concatenate([-values[..., CH:], values[..., :CH]], axis=-1)


def upper_blocks(edged, mask_rows):
    bin_count = edged.shape[0] - 2
    rotated = rotate(edged)
    snap = jnp.concatenate([edged[b : b + bin_count] for b in range(3)], axis=-1)
    turned_snap = jnp.concatenate([rotated[b : b + bin_count] for b in range(3)], axis=-1)
    both = jnp.concatenate([snap, turned_snap], axis=1)
    weighting = jnp.concatenate([mask_rows, mask_rows], axis=1)[:, :, None]
    masked = both * weighting
    pieces = []
    for left_pos in range(3):
        pieces.append(
            jnp.einsum(
                "krn,krm->knm",
                masked[:, :, left_pos * 2 * CH : left_pos * 2 * CH + CH],
                both[:, :, left_pos * 2 * CH :],
                preferred_element_type=jnp.float32,
            )
        )
    return jnp.concatenate(pieces, axis=-1)


def eliminate(parts_ref, steer_ref, unit_ref, wr_ref, wi_ref):
    rows, cols = wr_ref.shape
    gap = cols - LOOKS
    lane_ids = lax.broadcasted_iota(jnp.int32, (1, cols), 1)
    row_ids = lax.broadcasted_iota(jnp.int32, (rows, 1), 0)
    diagonal = row_ids == lax.broadcasted_iota(jnp.int32, (1, rows), 1)
    same = parts_ref[0, 0]
    power = 2.0 * jnp.sum(jnp.where(diagonal, same, 0.0)) / SNAP + epsilon
    steer = steer_ref[...]
    steer_re = jnp.concatenate([steer[2 * b * CH : (2 * b + 1) * CH] for b in range(rows // CH)], 0)
    steer_im = jnp.concatenate([steer[(2 * b + 1) * CH : (2 * b + 2) * CH] for b in range(rows // CH)], 0)
    wr_ref[...] = jnp.zeros(wr_ref.shape, jnp.float32)
    wi_ref[...] = jnp.zeros(wi_ref.shape, jnp.float32)
    wr_ref[:, :rows] = same / power + jnp.where(diagonal, loading, 0.0)
    wi_ref[:, :rows] = parts_ref[0, 1] / power
    wr_ref[:, gap:] = steer_re
    wi_ref[:, gap:] = steer_im

    def pick(values, hit):
        return jnp.sum(jnp.where(hit, values, 0.0), axis=1, keepdims=True)

    def times(a_r, a_i, b_r, b_i):
        return a_r * b_r - a_i * b_i, a_r * b_i + a_i * b_r

    def step(half, carry):
        j = 2 * half
        cur_r = wr_ref[...]
        cur_i = wi_ref[...]
        top_r = wr_ref[pl.ds(j, 1), :]
        top_i = wi_ref[pl.ds(j, 1), :]
        low_r = wr_ref[pl.ds(j + 1, 1), :]
        low_i = wi_ref[pl.ds(j + 1, 1), :]
        first = lane_ids == j
        second = lane_ids == j + 1
        a_r, a_i = pick(top_r, first), pick(top_i, first)
        b_r, b_i = pick(top_r, second), pick(top_i, second)
        c_r, c_i = pick(low_r, first), pick(low_i, first)
        d_r, d_i = pick(low_r, second), pick(low_i, second)
        ad_r, ad_i = times(a_r, a_i, d_r, d_i)
        bc_r, bc_i = times(b_r, b_i, c_r, c_i)
        det_r, det_i = ad_r - bc_r, ad_i - bc_i
        scale = 1.0 / (det_r * det_r + det_i * det_i)
        inv_r, inv_i = det_r * scale, -det_i * scale
        p_r, p_i = times(d_r, d_i, top_r, top_i)
        q_r, q_i = times(b_r, b_i, low_r, low_i)
        one_r, one_i = times(inv_r, inv_i, p_r - q_r, p_i - q_i)
        s_r, s_i = times(a_r, a_i, low_r, low_i)
        t_r, t_i = times(c_r, c_i, top_r, top_i)
        two_r, two_i = times(inv_r, inv_i, s_r - t_r, s_i - t_i)
        u_r, u_i = pick(cur_r, first), pick(cur_i, first)
        v_r, v_i = pick(cur_r, second), pick(cur_i, second)
        x_r, x_i = times(u_r, u_i, one_r, one_i)
        y_r, y_i = times(v_r, v_i, two_r, two_i)
        wr_ref[...] = cur_r - (x_r + y_r)
        wi_ref[...] = cur_i - (x_i + y_i)
        wr_ref[pl.ds(j, 1), :] = one_r
        wi_ref[pl.ds(j, 1), :] = one_i
        wr_ref[pl.ds(j + 1, 1), :] = two_r
        wi_ref[pl.ds(j + 1, 1), :] = two_i
        return carry

    lax.fori_loop(0, rows // 2, step, 0)
    solved_re = wr_ref[:, gap:]
    solved_im = wi_ref[:, gap:]
    root = jnp.sqrt(jnp.sum(steer_re * solved_re + steer_im * solved_im, axis=0, keepdims=True))
    unit_re = (solved_re / root).astype(unit_ref.dtype)
    unit_im = (solved_im / root).astype(unit_ref.dtype)
    for pos in range(rows // CH):
        unit_ref[0, 2 * pos * CH : (2 * pos + 1) * CH, :] = unit_re[pos * CH : (pos + 1) * CH]
        unit_ref[0, (2 * pos + 1) * CH : (2 * pos + 2) * CH, :] = unit_im[pos * CH : (pos + 1) * CH]

def unit_vectors(same, cross, steer):
    count, size, _ = same.shape
    parts = jnp.stack([same, cross], axis=1)
    width = ((size + 127) // 128) * 128 + LOOKS
    vector = pl.BlockSpec((2 * size, LOOKS), lambda i: (0, 0))
    return pl.pallas_call(
        eliminate,
        grid=(count,),
        in_specs=[pl.BlockSpec((1, 2, size, size), lambda i: (i, 0, 0, 0)), vector],
        out_specs=pl.BlockSpec((1, 2 * size, LOOKS), lambda i: (i, 0, 0)),
        out_shape=jax.ShapeDtypeStruct((count, 2 * size, LOOKS), jnp.bfloat16),
        scratch_shapes=[pltpu.VMEM((size, width), jnp.float32)] * 2,
    )(parts, steer)


def hermitian_parts(upper):
    def piece(left_pos, right_pos):
        start = block_pairs.index((left_pos, right_pos)) * 2 * CH
        return upper[:, :, start : start + 2 * CH]

    def real_block(left_pos, right_pos):
        if left_pos > right_pos:
            return jnp.swapaxes(real_block(right_pos, left_pos), 1, 2)
        return piece(left_pos, right_pos)[..., :CH]

    def imag_block(left_pos, right_pos):
        if left_pos > right_pos:
            return -jnp.swapaxes(imag_block(right_pos, left_pos), 1, 2)
        return -piece(left_pos, right_pos)[..., CH:]

    def assemble(block):
        rows = [jnp.concatenate([block(b, c) for c in range(3)], -1) for b in range(3)]
        return jnp.concatenate(rows, 1)

    return assemble(real_block), assemble(imag_block)


def body(echoes, training, look_index):
    spectra = doppler_spectra(echoes, twiddles())
    turned = lax.all_to_all(spectra, "dop", split_axis=0, concat_axis=1, tiled=True)
    turned = turned.reshape(turned.shape[0], -1, 2 * CH)
    edged = padded(turned, (("dop", 0),), 1)
    bin_count = edged.shape[0] - 2
    upper = upper_blocks(edged, training.astype(jnp.bfloat16))
    my_upper = sum_at_owner(upper, "rng", 0)
    my_unit = unit_vectors(*hermitian_parts(my_upper), steering(look_index))
    unit = gather_directly(my_unit, "rng", 0)
    shaped = unit.reshape(bin_count, 3, 2, CH, LOOKS)
    rotated = jnp.stack([-shaped[:, :, 1], shaped[:, :, 0]], axis=2).reshape(bin_count, SNAP, LOOKS)
    weights = jnp.concatenate([unit, rotated], axis=2)
    summed = None
    for position in range(3):
        term = jnp.einsum(
            "knj,krn->kjr",
            weights[:, position * 2 * CH : (position + 1) * 2 * CH],
            edged[position : position + bin_count],
            preferred_element_type=jnp.float32,
        )
        summed = term if summed is None else summed + term
    return summed.reshape(bin_count, 2, LOOKS, edged.shape[1])


def solution(mesh):
    in_specs = (P(("rng", "dop"), None, None, None), P("dop", "rng"), P())
    out_specs = P("dop", None, None, "rng")
    return jax.shard_map(body, mesh=mesh, in_specs=in_specs, out_specs=out_specs, check_vma=False)
```
